128 devices in a mesh: rep: 4 (over x), fsdp: 2 (over core), tp: 16 (over z, y).
Axes of the slice: x: 4, y: 4, z: 4, core: 2. Of those that a mesh axis runs over, the one named last changes fastest.
Arguments:
- tokens: bfloat16 [8192, 2048], P(('rep', 'fsdp'), 'tp'), may hold values from -6 to 6
- cotangent: bfloat16 [8192, 2048], P(('rep', 'fsdp'), 'tp'), may hold values from -6 to 6
- frame_mask: int32 [8192], P(('rep', 'fsdp')), may hold values 0 or 1
- ln_gain: bfloat16 [2048], P('tp'), may hold values from 0.099609375 to 1.8984375
- ln_bias: bfloat16 [2048], P('tp'), may hold values from -3 to 3
- weight_in: bfloat16 [2048, 8192], P('fsdp', 'tp'), may hold values from -0.1875 to 0.1875
- weight_out: bfloat16 [8192, 2048], P('tp', 'fsdp'), may hold values from -0.09375 to 0.09375
- blocks_in: int32 [16, 64], P('fsdp', 'tp'), may hold values 0 or 1
- blocks_out: int32 [64, 16], P('tp', 'fsdp'), may hold values 0 or 1
Outputs:
- block_out: bfloat16 [8192, 2048], P(('rep', 'fsdp'), 'tp')
- input_grad: bfloat16 [8192, 2048], P(('rep', 'fsdp'), 'tp')
- grad_in: float32 [2048, 8192], P('fsdp', 'tp')
- grad_out: float32 [8192, 2048], P('tp', 'fsdp')
- grad_gain: float32 [2048], P('tp')
- grad_bias: float32 [2048], P('tp')
The draws below stay inside these ranges and needn't reach their ends.
All inputs are finite; a program needn't handle non-finite values. No bound on the sum of `frame_mask` or of `blocks_in` or of `blocks_out` on one device may be relied on, other than what follows from the above.
Results may differ from the reference program's by a relative error of at most 0.019.
Values may be sent and summed in bfloat16 or wider, within the bound.
No kernel may reach another device: no remote copies, remote signals or barrier semaphores. Data moves between devices by JAX's collectives and lax.ppermute only.
A program may use at most 128 MiB of HBM per device.

```python
from functools import partial
import jax
import jax.numpy as jnp
from jax import lax

D = 2048
FF = 8192
BLK = 128
TOK_DEV = 1024
TOKENS = 8192
N_REP = 4
N_FSDP = 2
N_TP = 16


def plant(result, own_key, smallest, high):
    longest = result.shape.index(max(result.shape))
    spots = []
    for shift in (0, 1):
        where = [jax.random.randint(jax.random.fold_in(own_key, axis), (), 0, length) for axis, length in enumerate(result.shape)]
        where[longest] = (where[longest] + shift) % result.shape[longest]
        spots.append(tuple(where))
    return result.at[spots[0]].set(smallest).at[spots[1]].set(high)


def level_of(rng, shape, cuts, smallest, largest):
    level = 1.0
    for dim, blocks in cuts:
        steps = jax.random.uniform(jax.random.fold_in(jax.random.fold_in(rng, 6), dim), (blocks,), jnp.float32, smallest / len(cuts), largest / len(cuts))
        level = level * jnp.repeat(jnp.exp(steps), shape[dim] // blocks).reshape((-1,) + (1,) * (len(shape) - 1 - dim))
    return level


def normal_values(key, extent, width, reach, cuts=(), kind=jnp.bfloat16):
    factor_of = level_of(key, extent, cuts, -0.22, 0.18) if cuts else 1.0
    result = jax.random.normal(key, extent, jnp.float32) * width * factor_of
    return jnp.minimum(jnp.maximum(result, -reach), reach).astype(kind)


def setup_inputs(seed: int = 0) -> dict:
    seeds = jax.random.split(jax.random.key(seed), 10)
    return {
        "tokens": normal_values(seeds[0], (TOKENS, D), 1.0, 6.0, ((0, 8), (1, 16))),
        "cotangent": normal_values(seeds[1], (TOKENS, D), 1.0, 6.0, ((0, 8), (1, 16))),
        "frame_mask": plant((jax.random.randint(seeds[2], (TOKENS,), 0, 2) < 1).astype(jnp.int32), jax.random.fold_in(seeds[2], 1), 0, 1),
        "ln_gain": jnp.clip(1.0 + 0.18 * jax.random.normal(seeds[3], (D,), jnp.float32), 0.099609375, 1.8984375).astype(jnp.bfloat16),
        "ln_bias": normal_values(seeds[4], (D,), 0.5, 3.0, ((0, 16),)),
        "weight_in": normal_values(seeds[5], (D, FF), (D // 2) ** -0.5, 0.1875, ((0, 2), (1, 16))),
        "weight_out": normal_values(seeds[6], (FF, D), (FF // 2) ** -0.5, 0.09375, ((0, 16), (1, 2))),
        "blocks_in": plant((jax.random.randint(seeds[7], (D // BLK, FF // BLK), 0, 2) < 1).astype(jnp.int32), jax.random.fold_in(seeds[7], 1), 0, 1),
        "blocks_out": plant((jax.random.randint(seeds[8], (FF // BLK, D // BLK), 0, 2) < 1).astype(jnp.int32), jax.random.fold_in(seeds[8], 1), 0, 1),
    }


def spread_blocks(blocks):
    return jnp.repeat(jnp.repeat(blocks, BLK, axis=0), BLK, axis=1)

def round_keep(array):
    return lax.optimization_barrier(array.astype(jnp.bfloat16)).astype(jnp.float32)

def reference(tokens, cotangent, frame_mask, ln_gain, ln_bias, weight_in, weight_out, blocks_in, blocks_out):
    groups = N_REP * N_FSDP
    local_cols = FF // N_TP
    masked_in = weight_in * spread_blocks(blocks_in).astype(jnp.bfloat16)
    masked_out = weight_out * spread_blocks(blocks_out).astype(jnp.bfloat16)
    gain_full = ln_gain.astype(jnp.float32)
    bias_full = ln_bias.astype(jnp.float32)
    gelu_exact = partial(jax.nn.gelu, approximate=False)
    split_in = masked_in.astype(jnp.float32).reshape(D, N_TP, local_cols)
    split_out = masked_out.astype(jnp.float32).reshape(N_TP, local_cols, D)

    def per_group(totals, inputs):
        sum_in, sum_out, sum_gain, sum_bias = totals
        token_rows, upstream, frame_flags = inputs
        values = token_rows.astype(jnp.float32)
        centre = lax.optimization_barrier(jnp.mean(values, axis=1, keepdims=True))
        centred = values - centre
        inv_std = lax.rsqrt(lax.optimization_barrier(jnp.mean(centred * centred, axis=1, keepdims=True)) + 1e-05)
        normed = centred * inv_std
        scaled = (normed * gain_full + bias_full).astype(jnp.bfloat16)
        hidden = jnp.dot(scaled, masked_in, preferred_element_type=jnp.float32)
        active = gelu_exact(hidden).astype(jnp.bfloat16)
        pieces = jnp.einsum('tkf,kfd->ktd', active.astype(jnp.float32).reshape(TOK_DEV, N_TP, local_cols), split_out)
        branch = lax.optimization_barrier(jnp.sum(round_keep(pieces), axis=0))
        output = (values + branch).astype(jnp.bfloat16)
        chosen = upstream * frame_flags[:, None].astype(jnp.bfloat16)
        back_active = jnp.dot(chosen, masked_out.T, preferred_element_type=jnp.float32)
        unused, gelu_back = jax.vjp(gelu_exact, hidden)
        back_hidden = gelu_back(back_active)[0].astype(jnp.bfloat16)
        pieces_in = jnp.einsum('tkf,dkf->ktd', back_hidden.astype(jnp.float32).reshape(TOK_DEV, N_TP, local_cols), split_in)
        back_normed = lax.optimization_barrier(jnp.sum(round_keep(pieces_in), axis=0))
        back_scaled = back_normed * gain_full
        mean_plain = lax.optimization_barrier(jnp.mean(back_scaled, axis=1, keepdims=True))
        mean_cross = lax.optimization_barrier(jnp.mean(back_scaled * normed, axis=1, keepdims=True))
        back_rows = inv_std * (back_scaled - mean_plain - normed * mean_cross)
        grad_rows = (chosen.astype(jnp.float32) + back_rows).astype(jnp.bfloat16)
        sum_gain = sum_gain + lax.optimization_barrier(jnp.sum(back_normed * normed, axis=0))
        sum_bias = sum_bias + lax.optimization_barrier(jnp.sum(back_normed, axis=0))
        term_in = jnp.dot(scaled.T, back_hidden, preferred_element_type=jnp.float32)
        term_out = jnp.dot(active.T, chosen, preferred_element_type=jnp.float32)
        sum_in = sum_in + round_keep(term_in)
        sum_out = sum_out + round_keep(term_out)
        return ((sum_in, sum_out, sum_gain, sum_bias), (output, grad_rows))
    start = (jnp.zeros((D, FF), jnp.float32), jnp.zeros((FF, D), jnp.float32), jnp.zeros((D,), jnp.float32), jnp.zeros((D,), jnp.float32))
    inputs = (tokens.reshape(groups, TOK_DEV, D), cotangent.reshape(groups, TOK_DEV, D), frame_mask.reshape(groups, TOK_DEV))
    totals, stacked = lax.scan(per_group, start, inputs)
    sum_in, sum_out, sum_gain, sum_bias = totals
    grad_in = sum_in * spread_blocks(blocks_in).astype(jnp.float32)
    grad_out = sum_out * spread_blocks(blocks_out).astype(jnp.float32)
    block_out = stacked[0].reshape(TOKENS, D)
    input_grad = stacked[1].reshape(TOKENS, D)
    return (block_out, input_grad, grad_in, grad_out, sum_gain, sum_bias)
```

```python
from functools import partial

import jax
import jax.numpy as jnp
from jax import lax
from jax.sharding import PartitionSpec as P

BLK = 128


def apply_blocks(weight, blocks, kind):
    row_blocks, col_blocks = blocks.shape
    shaped = weight.reshape(row_blocks, BLK, col_blocks, BLK)
    keeper = blocks.astype(kind)[:, None, :, None]
    return (shaped * keeper).reshape(weight.shape)


def contract_rows(left, right):
    return lax.dot_general(
        left, right, (((0,), (0,)), ((), ())), preferred_element_type=jnp.float32
    )


def contract_cols(left, right):
    return lax.dot_general(
        left, right, (((1,), (1,)), ((), ())), preferred_element_type=jnp.float32
    )


def pair_gather(own, axis):
    other = lax.ppermute(own, "fsdp", perm=[(0, 1), (1, 0)])
    first = lax.axis_index("fsdp") == 0
    low = jnp.where(first, own, other)
    high = jnp.where(first, other, own)
    return jnp.concatenate([low, high], axis=axis)


def pair_scatter(term, axis):
    half = term.shape[axis] // 2
    idx = lax.axis_index("fsdp")
    keep = lax.dynamic_slice_in_dim(term, idx * half, half, axis)
    send = lax.dynamic_slice_in_dim(term, (1 - idx) * half, half, axis)
    recv = lax.ppermute(send, "fsdp", perm=[(0, 1), (1, 0)])
    return keep.astype(jnp.float32) + recv.astype(jnp.float32)


def ring_allreduce(flat, axis, size):
    me = lax.axis_index(axis)
    halves = flat.reshape(2, size, -1)
    fwd = [(i, (i + 1) % size) for i in range(size)]
    bwd = [(i, (i - 1) % size) for i in range(size)]
    parts = []
    for direction, perm in ((1, fwd), (-1, bwd)):
        chunks = halves[0 if direction == 1 else 1]
        acc = lax.dynamic_index_in_dim(chunks, me % size, 0, keepdims=False)
        for step in range(size - 1):
            recv = lax.ppermute(acc.astype(jnp.bfloat16), axis, perm=perm)
            src = (me - direction * (step + 1)) % size
            acc = recv.astype(jnp.float32) + lax.dynamic_index_in_dim(
                chunks, src, 0, keepdims=False
            )
        owned = (me - direction * (size - 1)) % size
        out = jnp.zeros((size,) + acc.shape, jnp.float32)
        piece = acc.astype(jnp.bfloat16)
        out = lax.dynamic_update_index_in_dim(out, piece.astype(jnp.float32), owned, 0)
        for step in range(size - 1):
            piece = lax.ppermute(piece, axis, perm=perm)
            slot = (owned - direction * (step + 1)) % size
            out = lax.dynamic_update_index_in_dim(out, piece.astype(jnp.float32), slot, 0)
        parts.append(out)
    return jnp.stack(parts).reshape(flat.shape)


def on_device(
    n_rep,
    tokens, cotangent, frame_mask, ln_gain, ln_bias, weight_in, weight_out, blocks_in, blocks_out
):
    params = lax.all_gather(jnp.stack([ln_gain, ln_bias]), "tp", axis=1, tiled=True)
    gain_full, bias_full = params[0], params[1]
    whole_rows = lax.all_gather(tokens, "tp", axis=1, tiled=True)
    masked_in = apply_blocks(weight_in, blocks_in, jnp.bfloat16)
    masked_out = apply_blocks(weight_out, blocks_out, jnp.bfloat16)
    full_in = pair_gather(masked_in, 0)
    full_out = pair_gather(masked_out, 1)
    width = whole_rows.shape[1]
    own_width = tokens.shape[1]
    col_start = lax.axis_index("tp") * own_width
    gelu_exact = partial(jax.nn.gelu, approximate=False)
    values = whole_rows.astype(jnp.float32)
    centre = jnp.mean(values, axis=1, keepdims=True)
    centred = values - centre
    inv_std = lax.rsqrt(jnp.mean(centred * centred, axis=1, keepdims=True) + 1e-05)
    normed = centred * inv_std
    gain_f = gain_full.astype(jnp.float32)
    scaled = (normed * gain_f + bias_full.astype(jnp.float32)).astype(jnp.bfloat16)
    hidden = jnp.dot(scaled, full_in, preferred_element_type=jnp.float32)
    active = gelu_exact(hidden).astype(jnp.bfloat16)
    partial_out = jnp.dot(active, full_out, preferred_element_type=jnp.float32)
    branch = lax.psum_scatter(
        partial_out.astype(jnp.bfloat16), "tp", scatter_dimension=1, tiled=True
    ).astype(jnp.float32)
    block_out = (tokens.astype(jnp.float32) + branch).astype(jnp.bfloat16)
    whole_grad = lax.all_gather(cotangent, "tp", axis=1, tiled=True)
    flags = frame_mask[:, None].astype(jnp.bfloat16)
    chosen = whole_grad * flags
    chosen_own = cotangent * flags
    back_active = contract_cols(chosen, full_out)
    unused, gelu_back = jax.vjp(gelu_exact, hidden)
    back_hidden = gelu_back(back_active)[0].astype(jnp.bfloat16)
    partial_normed = contract_cols(back_hidden, full_in).astype(jnp.bfloat16)
    piece = partial_normed.astype(jnp.float32)
    piece_scaled = piece * gain_f
    sum_plain, sum_cross = lax.psum(
        (jnp.sum(piece_scaled, axis=1), jnp.sum(piece_scaled * normed, axis=1)), "tp"
    )
    whole_gain, whole_bias = lax.psum(
        (jnp.sum(piece * normed, axis=0), jnp.sum(piece, axis=0)), ("rep", "fsdp", "tp")
    )
    grad_gain = lax.dynamic_slice_in_dim(whole_gain, col_start, own_width, 0)
    grad_bias = lax.dynamic_slice_in_dim(whole_bias, col_start, own_width, 0)
    back_normed = lax.psum_scatter(
        partial_normed, "tp", scatter_dimension=1, tiled=True
    ).astype(jnp.float32)
    normed_own = lax.dynamic_slice_in_dim(normed, col_start, own_width, 1)
    gain_own = ln_gain.astype(jnp.float32)
    back_scaled = back_normed * gain_own
    mean_plain = (sum_plain / width)[:, None]
    mean_cross = (sum_cross / width)[:, None]
    back_rows = inv_std * (back_scaled - mean_plain - normed_own * mean_cross)
    input_grad = (chosen_own.astype(jnp.float32) + back_rows).astype(jnp.bfloat16)
    term_in = contract_rows(scaled, back_hidden).astype(jnp.bfloat16)
    term_out = contract_rows(active, chosen).astype(jnp.bfloat16)
    shard_in = pair_scatter(term_in, 0)
    shard_out = pair_scatter(term_out, 1)
    both = jnp.concatenate([shard_in.reshape(-1), shard_out.reshape(-1)])
    total = ring_allreduce(both, "rep", n_rep)
    shard_in = total[: shard_in.size].reshape(shard_in.shape)
    shard_out = total[shard_in.size :].reshape(shard_out.shape)
    grad_in = apply_blocks(shard_in, blocks_in, jnp.float32)
    grad_out = apply_blocks(shard_out, blocks_out, jnp.float32)
    return (block_out, input_grad, grad_in, grad_out, grad_gain, grad_bias)


def solution(mesh):
    placed = (
        P(("rep", "fsdp"), "tp"),
        P(("rep", "fsdp"), "tp"),
        P(("rep", "fsdp")),
        P("tp"),
        P("tp"),
        P("fsdp", "tp"),
        P("tp", "fsdp"),
        P("fsdp", "tp"),
        P("tp", "fsdp"),
    )
    return jax.shard_map(
        partial(on_device, mesh.shape["rep"]),
        mesh=mesh,
        in_specs=placed,
        out_specs=(
            P(("rep", "fsdp"), "tp"),
            P(("rep", "fsdp"), "tp"),
            P("fsdp", "tp"),
            P("tp", "fsdp"),
            P("tp"),
            P("tp"),
        ),
        check_vma=False,
    )
```

```python
from functools import partial

import jax
import jax.numpy as jnp
from jax import lax
from jax.sharding import PartitionSpec as P

BLK = 128


def apply_blocks(weight, blocks, kind):
    row_blocks, col_blocks = blocks.shape
    shaped = weight.reshape(row_blocks, BLK, col_blocks, BLK)
    keeper = blocks.astype(kind)[:, None, :, None]
    return (shaped * keeper).reshape(weight.shape)


def contract_rows(left, right):
    return lax.dot_general(
        left, right, (((0,), (0,)), ((), ())), preferred_element_type=jnp.float32
    )


def contract_cols(left, right):
    return lax.dot_general(
        left, right, (((1,), (1,)), ((), ())), preferred_element_type=jnp.float32
    )


def pair_gather(own, axis):
    other = lax.ppermute(own, "fsdp", perm=[(0, 1), (1, 0)])
    first = lax.axis_index("fsdp") == 0
    low = jnp.where(first, own, other)
    high = jnp.where(first, other, own)
    return jnp.concatenate([low, high], axis=axis)


def pair_scatter(term, axis):
    half = term.shape[axis] // 2
    idx = lax.axis_index("fsdp")
    keep = lax.dynamic_slice_in_dim(term, idx * half, half, axis)
    send = lax.dynamic_slice_in_dim(term, (1 - idx) * half, half, axis)
    recv = lax.ppermute(send, "fsdp", perm=[(0, 1), (1, 0)])
    return keep.astype(jnp.float32) + recv.astype(jnp.float32)


def ring_allreduce(flat, axis, size):
    me = lax.axis_index(axis)
    halves = flat.reshape(2, size, -1)
    fwd = [(i, (i + 1) % size) for i in range(size)]
    bwd = [(i, (i - 1) % size) for i in range(size)]
    parts = []
    for direction, perm in ((1, fwd), (-1, bwd)):
        chunks = halves[0 if direction == 1 else 1]
        acc = lax.dynamic_index_in_dim(chunks, me % size, 0, keepdims=False)
        for step in range(size - 1):
            recv = lax.ppermute(acc.astype(jnp.bfloat16), axis, perm=perm)
            src = (me - direction * (step + 1)) % size
            acc = recv.astype(jnp.float32) + lax.dynamic_index_in_dim(
                chunks, src, 0, keepdims=False
            )
        owned = (me - direction * (size - 1)) % size
        pieces = [acc.astype(jnp.bfloat16)]
        for step in range(size - 1):
            pieces.append(lax.ppermute(pieces[-1], axis, perm=perm))
        slots = []
        for slot in range(size):
            pick = (direction * (owned - slot)) % size
            value = pieces[0]
            for j in range(1, size):
                value = jnp.where(pick == j, pieces[j], value)
            slots.append(value.astype(jnp.float32))
        parts.append(jnp.stack(slots))
    return jnp.stack(parts).reshape(flat.shape)


def butterfly_sum(values, axis, size):
    bit = 1
    while bit < size:
        perm = [(i, i ^ bit) for i in range(size)]
        values = values + lax.ppermute(values, axis, perm=perm)
        bit *= 2
    return values


def on_device(
    sizes,
    tokens, cotangent, frame_mask, ln_gain, ln_bias, weight_in, weight_out, blocks_in, blocks_out
):
    params = lax.all_gather(jnp.stack([ln_gain, ln_bias]), "tp", axis=1, tiled=True)
    gain_full, bias_full = params[0], params[1]
    whole_rows = lax.all_gather(tokens, "tp", axis=1, tiled=True)
    masked_in = apply_blocks(weight_in, blocks_in, jnp.bfloat16)
    masked_out = apply_blocks(weight_out, blocks_out, jnp.bfloat16)
    full_in = pair_gather(masked_in, 0)
    full_out = pair_gather(masked_out, 1)
    width = whole_rows.shape[1]
    own_width = tokens.shape[1]
    col_start = lax.axis_index("tp") * own_width
    gelu_exact = partial(jax.nn.gelu, approximate=False)
    values = whole_rows.astype(jnp.float32)
    centre = jnp.mean(values, axis=1, keepdims=True)
    centred = values - centre
    inv_std = lax.rsqrt(jnp.mean(centred * centred, axis=1, keepdims=True) + 1e-05)
    normed = centred * inv_std
    gain_f = gain_full.astype(jnp.float32)
    scaled = (normed * gain_f + bias_full.astype(jnp.float32)).astype(jnp.bfloat16)
    hidden = jnp.dot(scaled, full_in, preferred_element_type=jnp.float32)
    active = gelu_exact(hidden).astype(jnp.bfloat16)
    partial_out = jnp.dot(active, full_out, preferred_element_type=jnp.float32)
    branch = lax.psum_scatter(
        partial_out.astype(jnp.bfloat16), "tp", scatter_dimension=1, tiled=True
    ).astype(jnp.float32)
    block_out = (tokens.astype(jnp.float32) + branch).astype(jnp.bfloat16)
    whole_grad = lax.all_gather(cotangent, "tp", axis=1, tiled=True)
    flags = frame_mask[:, None].astype(jnp.bfloat16)
    chosen = whole_grad * flags
    chosen_own = cotangent * flags
    back_active = contract_cols(chosen, full_out)
    unused, gelu_back = jax.vjp(gelu_exact, hidden)
    back_hidden = gelu_back(back_active)[0].astype(jnp.bfloat16)
    partial_normed = contract_cols(back_hidden, full_in).astype(jnp.bfloat16)
    piece = partial_normed.astype(jnp.float32)
    piece_scaled = piece * gain_f
    row_sums = butterfly_sum(
        jnp.stack([jnp.sum(piece_scaled, axis=1), jnp.sum(piece_scaled * normed, axis=1)]),
        "tp",
        sizes["tp"],
    )
    sum_plain, sum_cross = row_sums[0], row_sums[1]
    col_sums = jnp.stack([jnp.sum(piece * normed, axis=0), jnp.sum(piece, axis=0)])
    for name in ("tp", "fsdp", "rep"):
        col_sums = butterfly_sum(col_sums, name, sizes[name])
    whole_gain, whole_bias = col_sums[0], col_sums[1]
    grad_gain = lax.dynamic_slice_in_dim(whole_gain, col_start, own_width, 0)
    grad_bias = lax.dynamic_slice_in_dim(whole_bias, col_start, own_width, 0)
    back_normed = lax.psum_scatter(
        partial_normed, "tp", scatter_dimension=1, tiled=True
    ).astype(jnp.float32)
    normed_own = lax.dynamic_slice_in_dim(normed, col_start, own_width, 1)
    gain_own = ln_gain.astype(jnp.float32)
    back_scaled = back_normed * gain_own
    mean_plain = (sum_plain / width)[:, None]
    mean_cross = (sum_cross / width)[:, None]
    back_rows = inv_std * (back_scaled - mean_plain - normed_own * mean_cross)
    input_grad = (chosen_own.astype(jnp.float32) + back_rows).astype(jnp.bfloat16)
    term_in = contract_rows(scaled, back_hidden).astype(jnp.bfloat16)
    term_out = contract_rows(active, chosen).astype(jnp.bfloat16)
    shard_in = pair_scatter(term_in, 0)
    shard_out = pair_scatter(term_out, 1)
    both = jnp.concatenate([shard_in.reshape(-1), shard_out.reshape(-1)])
    total = ring_allreduce(both, "rep", sizes["rep"])
    shard_in = total[: shard_in.size].reshape(shard_in.shape)
    shard_out = total[shard_in.size :].reshape(shard_out.shape)
    grad_in = apply_blocks(shard_in, blocks_in, jnp.float32)
    grad_out = apply_blocks(shard_out, blocks_out, jnp.float32)
    return (block_out, input_grad, grad_in, grad_out, grad_gain, grad_bias)


def solution(mesh):
    placed = (
        P(("rep", "fsdp"), "tp"),
        P(("rep", "fsdp"), "tp"),
        P(("rep", "fsdp")),
        P("tp"),
        P("tp"),
        P("fsdp", "tp"),
        P("tp", "fsdp"),
        P("fsdp", "tp"),
        P("tp", "fsdp"),
    )
    return jax.shard_map(
        partial(on_device, dict(mesh.shape)),
        mesh=mesh,
        in_specs=placed,
        out_specs=(
            P(("rep", "fsdp"), "tp"),
            P(("rep", "fsdp"), "tp"),
            P("fsdp", "tp"),
            P("tp", "fsdp"),
            P("tp"),
            P("tp"),
        ),
        check_vma=False,
    )
```

```python
from functools import partial

import jax
import jax.numpy as jnp
from jax import lax
from jax.sharding import PartitionSpec as P

BLK = 128


def apply_blocks(weight, blocks, kind):
    row_blocks, col_blocks = blocks.shape
    shaped = weight.reshape(row_blocks, BLK, col_blocks, BLK)
    keeper = blocks.astype(kind)[:, None, :, None]
    return (shaped * keeper).reshape(weight.shape)


def contract_rows(left, right):
    return lax.dot_general(
        left, right, (((0,), (0,)), ((), ())), preferred_element_type=jnp.float32
    )


def contract_cols(left, right):
    return lax.dot_general(
        left, right, (((1,), (1,)), ((), ())), preferred_element_type=jnp.float32
    )


def pair_gather(own, axis):
    other = lax.ppermute(own, "fsdp", perm=[(0, 1), (1, 0)])
    first = lax.axis_index("fsdp") == 0
    low = jnp.where(first, own, other)
    high = jnp.where(first, other, own)
    return jnp.concatenate([low, high], axis=axis)


def pair_scatter(term, axis):
    half = term.shape[axis] // 2
    idx = lax.axis_index("fsdp")
    keep = lax.dynamic_slice_in_dim(term, idx * half, half, axis)
    send = lax.dynamic_slice_in_dim(term, (1 - idx) * half, half, axis)
    recv = lax.ppermute(send, "fsdp", perm=[(0, 1), (1, 0)])
    return keep.astype(jnp.float32) + recv.astype(jnp.float32)


def ring_allreduce(flat, axis, size):
    me = lax.axis_index(axis)
    halves = flat.reshape(2, size, -1)
    fwd = [(i, (i + 1) % size) for i in range(size)]
    bwd = [(i, (i - 1) % size) for i in range(size)]
    parts = []
    for direction, perm in ((1, fwd), (-1, bwd)):
        chunks = halves[0 if direction == 1 else 1]
        acc = lax.dynamic_index_in_dim(chunks, me % size, 0, keepdims=False)
        for step in range(size - 1):
            recv = lax.ppermute(acc.astype(jnp.bfloat16), axis, perm=perm)
            src = (me - direction * (step + 1)) % size
            acc = recv.astype(jnp.float32) + lax.dynamic_index_in_dim(
                chunks, src, 0, keepdims=False
            )
        owned = (me - direction * (size - 1)) % size
        pieces = [acc.astype(jnp.bfloat16)]
        for step in range(size - 1):
            pieces.append(lax.ppermute(pieces[-1], axis, perm=perm))
        values = [lax.reduce_precision(acc, exponent_bits=8, mantissa_bits=7)]
        values += [p.astype(jnp.float32) for p in pieces[1:]]
        slots = []
        for slot in range(size):
            pick = (direction * (owned - slot)) % size
            value = values[0]
            for j in range(1, size):
                value = jnp.where(pick == j, values[j], value)
            slots.append(value)
        parts.append(jnp.stack(slots))
    return jnp.stack(parts).reshape(flat.shape)


def butterfly_sum(values, axis, size):
    bit = 1
    while bit < size:
        perm = [(i, i ^ bit) for i in range(size)]
        values = values + lax.ppermute(values, axis, perm=perm)
        bit *= 2
    return values


def on_device(
    sizes,
    tokens, cotangent, frame_mask, ln_gain, ln_bias, weight_in, weight_out, blocks_in, blocks_out
):
    params = lax.all_gather(jnp.stack([ln_gain, ln_bias]), "tp", axis=1, tiled=True)
    gain_full, bias_full = params[0], params[1]
    whole_rows = lax.all_gather(tokens, "tp", axis=1, tiled=True)
    masked_in = apply_blocks(weight_in, blocks_in, jnp.bfloat16)
    masked_out = apply_blocks(weight_out, blocks_out, jnp.bfloat16)
    full_in = pair_gather(masked_in, 0)
    full_out = pair_gather(masked_out, 1)
    width = whole_rows.shape[1]
    own_width = tokens.shape[1]
    col_start = lax.axis_index("tp") * own_width
    gelu_exact = partial(jax.nn.gelu, approximate=False)
    values = whole_rows.astype(jnp.float32)
    centre = jnp.mean(values, axis=1, keepdims=True)
    centred = values - centre
    inv_std = lax.rsqrt(jnp.mean(centred * centred, axis=1, keepdims=True) + 1e-05)
    normed = centred * inv_std
    gain_f = gain_full.astype(jnp.float32)
    scaled = (normed * gain_f + bias_full.astype(jnp.float32)).astype(jnp.bfloat16)
    hidden = jnp.dot(scaled, full_in, preferred_element_type=jnp.float32)
    active = gelu_exact(hidden).astype(jnp.bfloat16)
    partial_out = jnp.dot(active, full_out, preferred_element_type=jnp.float32)
    partial_out = partial_out.astype(jnp.bfloat16)
    whole_grad = lax.all_gather(cotangent, "tp", axis=1, tiled=True)
    unused, whole_grad = lax.optimization_barrier((partial_out, whole_grad))
    branch = lax.psum_scatter(
        partial_out, "tp", scatter_dimension=1, tiled=True
    ).astype(jnp.float32)
    flags = frame_mask[:, None].astype(jnp.bfloat16)
    chosen = whole_grad * flags
    chosen_own = cotangent * flags
    back_active = contract_cols(chosen, full_out)
    unused, gelu_back = jax.vjp(gelu_exact, hidden)
    back_hidden = gelu_back(back_active)[0].astype(jnp.bfloat16)
    partial_normed = contract_cols(back_hidden, full_in).astype(jnp.bfloat16)
    back_normed = lax.psum_scatter(
        partial_normed, "tp", scatter_dimension=1, tiled=True
    ).astype(jnp.float32)
    piece = partial_normed.astype(jnp.float32)
    piece_scaled = piece * gain_f
    row_sums = butterfly_sum(
        jnp.stack([jnp.sum(piece_scaled, axis=1), jnp.sum(piece_scaled * normed, axis=1)]),
        "tp",
        sizes["tp"],
    )
    sum_plain, sum_cross = row_sums[0], row_sums[1]
    col_sums = jnp.stack([jnp.sum(piece * normed, axis=0), jnp.sum(piece, axis=0)])
    for name in ("tp", "fsdp", "rep"):
        col_sums = butterfly_sum(col_sums, name, sizes[name])
    whole_gain, whole_bias = col_sums[0], col_sums[1]
    grad_gain = lax.dynamic_slice_in_dim(whole_gain, col_start, own_width, 0)
    grad_bias = lax.dynamic_slice_in_dim(whole_bias, col_start, own_width, 0)
    term_in = contract_rows(scaled, back_hidden).astype(jnp.bfloat16)
    term_out = contract_rows(active, chosen).astype(jnp.bfloat16)
    shard_in = pair_scatter(term_in, 0)
    shard_out = pair_scatter(term_out, 1)
    both = jnp.concatenate([shard_in.reshape(-1), shard_out.reshape(-1)])
    both, branch = lax.optimization_barrier((both, branch))
    block_out = (tokens.astype(jnp.float32) + branch).astype(jnp.bfloat16)
    total = ring_allreduce(both, "rep", sizes["rep"])
    total, back_normed = lax.optimization_barrier((total, back_normed))
    shard_in = total[: shard_in.size].reshape(shard_in.shape)
    shard_out = total[shard_in.size :].reshape(shard_out.shape)
    normed_own = lax.dynamic_slice_in_dim(normed, col_start, own_width, 1)
    gain_own = ln_gain.astype(jnp.float32)
    back_scaled = back_normed * gain_own
    mean_plain = (sum_plain / width)[:, None]
    mean_cross = (sum_cross / width)[:, None]
    back_rows = inv_std * (back_scaled - mean_plain - normed_own * mean_cross)
    input_grad = (chosen_own.astype(jnp.float32) + back_rows).astype(jnp.bfloat16)
    grad_in = apply_blocks(shard_in, blocks_in, jnp.float32)
    grad_out = apply_blocks(shard_out, blocks_out, jnp.float32)
    return (block_out, input_grad, grad_in, grad_out, grad_gain, grad_bias)


def solution(mesh):
    placed = (
        P(("rep", "fsdp"), "tp"),
        P(("rep", "fsdp"), "tp"),
        P(("rep", "fsdp")),
        P("tp"),
        P("tp"),
        P("fsdp", "tp"),
        P("tp", "fsdp"),
        P("fsdp", "tp"),
        P("tp", "fsdp"),
    )
    return jax.shard_map(
        partial(on_device, dict(mesh.shape)),
        mesh=mesh,
        in_specs=placed,
        out_specs=(
            P(("rep", "fsdp"), "tp"),
            P(("rep", "fsdp"), "tp"),
            P("fsdp", "tp"),
            P("tp", "fsdp"),
            P("tp"),
            P("tp"),
        ),
        check_vma=False,
    )
```

```python
from functools import partial

import jax
import jax.numpy as jnp
from jax import lax
from jax.sharding import PartitionSpec as P

BLK = 128


def apply_blocks(weight, blocks, kind):
    row_blocks, col_blocks = blocks.shape
    shaped = weight.reshape(row_blocks, BLK, col_blocks, BLK)
    keeper = blocks.astype(kind)[:, None, :, None]
    return (shaped * keeper).reshape(weight.shape)


def contract_rows(left, right):
    return lax.dot_general(
        left, right, (((0,), (0,)), ((), ())), preferred_element_type=jnp.float32
    )


def contract_cols(left, right):
    return lax.dot_general(
        left, right, (((1,), (1,)), ((), ())), preferred_element_type=jnp.float32
    )


def pair_gather(own, axis):
    other = lax.ppermute(own, "fsdp", perm=[(0, 1), (1, 0)])
    first = lax.axis_index("fsdp") == 0
    low = jnp.where(first, own, other)
    high = jnp.where(first, other, own)
    return jnp.concatenate([low, high], axis=axis)


def pair_scatter(term, axis):
    half = term.shape[axis] // 2
    idx = lax.axis_index("fsdp")
    keep = lax.dynamic_slice_in_dim(term, idx * half, half, axis)
    send = lax.dynamic_slice_in_dim(term, (1 - idx) * half, half, axis)
    recv = lax.ppermute(send, "fsdp", perm=[(0, 1), (1, 0)])
    return keep.astype(jnp.float32) + recv.astype(jnp.float32)


def ring_allreduce(flat, axis, size):
    me = lax.axis_index(axis)
    halves = flat.reshape(2, size, -1)
    fwd = [(i, (i + 1) % size) for i in range(size)]
    bwd = [(i, (i - 1) % size) for i in range(size)]
    parts = []
    for direction, perm in ((1, fwd), (-1, bwd)):
        chunks = halves[0 if direction == 1 else 1]
        acc = lax.dynamic_index_in_dim(chunks, me % size, 0, keepdims=False)
        for step in range(size - 1):
            recv = lax.ppermute(acc.astype(jnp.bfloat16), axis, perm=perm)
            src = (me - direction * (step + 1)) % size
            acc = recv.astype(jnp.float32) + lax.dynamic_index_in_dim(
                chunks, src, 0, keepdims=False
            )
        owned = (me - direction * (size - 1)) % size
        pieces = [acc.astype(jnp.bfloat16)]
        for step in range(size - 1):
            pieces.append(lax.ppermute(pieces[-1], axis, perm=perm))
        values = [lax.reduce_precision(acc, exponent_bits=8, mantissa_bits=7)]
        values += [p.astype(jnp.float32) for p in pieces[1:]]
        slots = []
        for slot in range(size):
            pick = (direction * (owned - slot)) % size
            value = values[0]
            for j in range(1, size):
                value = jnp.where(pick == j, values[j], value)
            slots.append(value)
        parts.append(jnp.stack(slots))
    return jnp.stack(parts).reshape(flat.shape)


def butterfly_sum(values, axis, size):
    bit = 1
    while bit < size:
        perm = [(i, i ^ bit) for i in range(size)]
        values = values + lax.ppermute(values, axis, perm=perm)
        bit *= 2
    return values


def on_device(
    sizes,
    tokens, cotangent, frame_mask, ln_gain, ln_bias, weight_in, weight_out, blocks_in, blocks_out
):
    frames = tokens.shape[0]
    stacked = jnp.concatenate(
        [tokens, ln_gain[None], ln_bias[None], jnp.zeros((6, tokens.shape[1]), tokens.dtype)]
    )
    gathered = lax.all_to_all(
        jnp.tile(stacked, (1, sizes["tp"])), "tp", split_axis=1, concat_axis=1, tiled=True
    )
    whole_rows = gathered[:frames]
    gain_full, bias_full = gathered[frames], gathered[frames + 1]
    masked_in = apply_blocks(weight_in, blocks_in, jnp.bfloat16)
    masked_out = apply_blocks(weight_out, blocks_out, jnp.bfloat16)
    full_in = pair_gather(masked_in, 0)
    full_out = pair_gather(masked_out, 1)
    width = whole_rows.shape[1]
    own_width = tokens.shape[1]
    col_start = lax.axis_index("tp") * own_width
    gelu_exact = partial(jax.nn.gelu, approximate=False)
    values = whole_rows.astype(jnp.float32)
    centre = jnp.mean(values, axis=1, keepdims=True)
    centred = values - centre
    inv_std = lax.rsqrt(jnp.mean(centred * centred, axis=1, keepdims=True) + 1e-05)
    normed = centred * inv_std
    gain_f = gain_full.astype(jnp.float32)
    scaled = (normed * gain_f + bias_full.astype(jnp.float32)).astype(jnp.bfloat16)
    hidden = jnp.dot(scaled, full_in, preferred_element_type=jnp.float32)
    active = gelu_exact(hidden).astype(jnp.bfloat16)
    partial_out = jnp.dot(active, full_out, preferred_element_type=jnp.float32)
    partial_out = partial_out.astype(jnp.bfloat16)
    whole_grad = lax.all_gather(cotangent, "tp", axis=1, tiled=True)
    unused, whole_grad = lax.optimization_barrier((partial_out, whole_grad))
    branch = lax.psum_scatter(
        partial_out, "tp", scatter_dimension=1, tiled=True
    ).astype(jnp.float32)
    flags = frame_mask[:, None].astype(jnp.bfloat16)
    chosen = whole_grad * flags
    chosen_own = cotangent * flags
    back_active = contract_cols(chosen, full_out)
    unused, gelu_back = jax.vjp(gelu_exact, hidden)
    back_hidden = gelu_back(back_active)[0].astype(jnp.bfloat16)
    partial_normed = contract_cols(back_hidden, full_in).astype(jnp.bfloat16)
    back_normed = lax.psum_scatter(
        partial_normed, "tp", scatter_dimension=1, tiled=True
    ).astype(jnp.float32)
    piece = partial_normed.astype(jnp.float32)
    piece_scaled = piece * gain_f
    row_sums = butterfly_sum(
        jnp.stack([jnp.sum(piece_scaled, axis=1), jnp.sum(piece_scaled * normed, axis=1)]),
        "tp",
        sizes["tp"],
    )
    sum_plain, sum_cross = row_sums[0], row_sums[1]
    col_sums = jnp.stack([jnp.sum(piece * normed, axis=0), jnp.sum(piece, axis=0)])
    for name in ("tp", "fsdp", "rep"):
        col_sums = butterfly_sum(col_sums, name, sizes[name])
    whole_gain, whole_bias = col_sums[0], col_sums[1]
    grad_gain = lax.dynamic_slice_in_dim(whole_gain, col_start, own_width, 0)
    grad_bias = lax.dynamic_slice_in_dim(whole_bias, col_start, own_width, 0)
    term_in = contract_rows(scaled, back_hidden).astype(jnp.bfloat16)
    term_out = contract_rows(active, chosen).astype(jnp.bfloat16)
    shard_in = pair_scatter(term_in, 0)
    shard_out = pair_scatter(term_out, 1)
    both = jnp.concatenate([shard_in.reshape(-1), shard_out.reshape(-1)])
    both, branch = lax.optimization_barrier((both, branch))
    block_out = (tokens.astype(jnp.float32) + branch).astype(jnp.bfloat16)
    total = ring_allreduce(both, "rep", sizes["rep"])
    total, back_normed = lax.optimization_barrier((total, back_normed))
    shard_in = total[: shard_in.size].reshape(shard_in.shape)
    shard_out = total[shard_in.size :].reshape(shard_out.shape)
    normed_own = lax.dynamic_slice_in_dim(normed, col_start, own_width, 1)
    gain_own = ln_gain.astype(jnp.float32)
    back_scaled = back_normed * gain_own
    mean_plain = (sum_plain / width)[:, None]
    mean_cross = (sum_cross / width)[:, None]
    back_rows = inv_std * (back_scaled - mean_plain - normed_own * mean_cross)
    input_grad = (chosen_own.astype(jnp.float32) + back_rows).astype(jnp.bfloat16)
    grad_in = apply_blocks(shard_in, blocks_in, jnp.float32)
    grad_out = apply_blocks(shard_out, blocks_out, jnp.float32)
    return (block_out, input_grad, grad_in, grad_out, grad_gain, grad_bias)


def solution(mesh):
    placed = (
        P(("rep", "fsdp"), "tp"),
        P(("rep", "fsdp"), "tp"),
        P(("rep", "fsdp")),
        P("tp"),
        P("tp"),
        P("fsdp", "tp"),
        P("tp", "fsdp"),
        P("fsdp", "tp"),
        P("tp", "fsdp"),
    )
    return jax.shard_map(
        partial(on_device, dict(mesh.shape)),
        mesh=mesh,
        in_specs=placed,
        out_specs=(
            P(("rep", "fsdp"), "tp"),
            P(("rep", "fsdp"), "tp"),
            P("fsdp", "tp"),
            P("tp", "fsdp"),
            P("tp"),
            P("tp"),
        ),
        check_vma=False,
    )
```

```python
from functools import partial

import jax
import jax.numpy as jnp
from jax import lax
from jax.sharding import PartitionSpec as P

BLK = 128


def apply_blocks(weight, blocks, kind):
    row_blocks, col_blocks = blocks.shape
    shaped = weight.reshape(row_blocks, BLK, col_blocks, BLK)
    keeper = blocks.astype(kind)[:, None, :, None]
    return (shaped * keeper).reshape(weight.shape)


def contract_rows(left, right):
    return lax.dot_general(
        left, right, (((0,), (0,)), ((), ())), preferred_element_type=jnp.float32
    )


def contract_cols(left, right):
    return lax.dot_general(
        left, right, (((1,), (1,)), ((), ())), preferred_element_type=jnp.float32
    )


def pair_gather(own, axis):
    other = lax.ppermute(own, "fsdp", perm=[(0, 1), (1, 0)])
    first = lax.axis_index("fsdp") == 0
    low = jnp.where(first, own, other)
    high = jnp.where(first, other, own)
    return jnp.concatenate([low, high], axis=axis)


def pair_scatter(term, axis):
    half = term.shape[axis] // 2
    idx = lax.axis_index("fsdp")
    keep = lax.dynamic_slice_in_dim(term, idx * half, half, axis)
    send = lax.dynamic_slice_in_dim(term, (1 - idx) * half, half, axis)
    recv = lax.ppermute(send, "fsdp", perm=[(0, 1), (1, 0)])
    return keep.astype(jnp.float32) + recv.astype(jnp.float32)


def ring_allreduce(flat, axis, size):
    me = lax.axis_index(axis)
    halves = flat.reshape(2, size, -1)
    fwd = [(i, (i + 1) % size) for i in range(size)]
    bwd = [(i, (i - 1) % size) for i in range(size)]
    parts = []
    for direction, perm in ((1, fwd), (-1, bwd)):
        chunks = halves[0 if direction == 1 else 1]
        acc = lax.dynamic_index_in_dim(chunks, me % size, 0, keepdims=False)
        for step in range(size - 1):
            recv = lax.ppermute(acc.astype(jnp.bfloat16), axis, perm=perm)
            src = (me - direction * (step + 1)) % size
            acc = recv.astype(jnp.float32) + lax.dynamic_index_in_dim(
                chunks, src, 0, keepdims=False
            )
        owned = (me - direction * (size - 1)) % size
        pieces = [acc.astype(jnp.bfloat16)]
        for step in range(size - 1):
            pieces.append(lax.ppermute(pieces[-1], axis, perm=perm))
        values = [lax.reduce_precision(acc, exponent_bits=8, mantissa_bits=7)]
        values += [p.astype(jnp.float32) for p in pieces[1:]]
        slots = []
        for slot in range(size):
            pick = (direction * (owned - slot)) % size
            value = values[0]
            for j in range(1, size):
                value = jnp.where(pick == j, values[j], value)
            slots.append(value)
        parts.append(jnp.stack(slots))
    return jnp.stack(parts).reshape(flat.shape)


def butterfly_sum(values, axis, size):
    bit = 1
    while bit < size:
        perm = [(i, i ^ bit) for i in range(size)]
        values = values + lax.ppermute(values, axis, perm=perm)
        bit *= 2
    return values


def on_device(
    sizes,
    tokens, cotangent, frame_mask, ln_gain, ln_bias, weight_in, weight_out, blocks_in, blocks_out
):
    frames = tokens.shape[0]
    stacked = jnp.concatenate(
        [tokens, ln_gain[None], ln_bias[None], jnp.zeros((6, tokens.shape[1]), tokens.dtype)]
    )
    gathered = lax.all_to_all(
        jnp.tile(stacked, (1, sizes["tp"])), "tp", split_axis=1, concat_axis=1, tiled=True
    )
    whole_rows = gathered[:frames]
    gain_full, bias_full = gathered[frames], gathered[frames + 1]
    masked_in = apply_blocks(weight_in, blocks_in, jnp.bfloat16)
    masked_out = apply_blocks(weight_out, blocks_out, jnp.bfloat16)
    full_in = pair_gather(masked_in, 0)
    full_out = pair_gather(masked_out, 1)
    width = whole_rows.shape[1]
    own_width = tokens.shape[1]
    col_start = lax.axis_index("tp") * own_width
    gelu_exact = partial(jax.nn.gelu, approximate=False)
    values = whole_rows.astype(jnp.float32)
    centre = jnp.mean(values, axis=1, keepdims=True)
    centred = values - centre
    inv_std = lax.rsqrt(jnp.mean(centred * centred, axis=1, keepdims=True) + 1e-05)
    normed = centred * inv_std
    gain_f = gain_full.astype(jnp.float32)
    scaled = (normed * gain_f + bias_full.astype(jnp.float32)).astype(jnp.bfloat16)
    hidden = jnp.dot(scaled, full_in, preferred_element_type=jnp.float32)
    active = gelu_exact(hidden).astype(jnp.bfloat16)
    partial_out = jnp.dot(active, full_out, preferred_element_type=jnp.float32)
    partial_out = partial_out.astype(jnp.bfloat16)
    whole_grad = lax.all_gather(cotangent, "tp", axis=1, tiled=True)
    unused, whole_grad = lax.optimization_barrier((partial_out, whole_grad))
    received = lax.all_to_all(partial_out, "tp", split_axis=1, concat_axis=0, tiled=True)
    branch = jnp.sum(
        received.reshape(sizes["tp"], frames, -1).astype(jnp.float32), axis=0
    )
    flags = frame_mask[:, None].astype(jnp.bfloat16)
    chosen = whole_grad * flags
    chosen_own = cotangent * flags
    back_active = contract_cols(chosen, full_out)
    unused, gelu_back = jax.vjp(gelu_exact, hidden)
    back_hidden = gelu_back(back_active)[0].astype(jnp.bfloat16)
    partial_normed = contract_cols(back_hidden, full_in).astype(jnp.bfloat16)
    back_normed = lax.psum_scatter(
        partial_normed, "tp", scatter_dimension=1, tiled=True
    ).astype(jnp.float32)
    piece = partial_normed.astype(jnp.float32)
    piece_scaled = piece * gain_f
    row_sums = butterfly_sum(
        jnp.stack([jnp.sum(piece_scaled, axis=1), jnp.sum(piece_scaled * normed, axis=1)]),
        "tp",
        sizes["tp"],
    )
    sum_plain, sum_cross = row_sums[0], row_sums[1]
    col_sums = jnp.stack([jnp.sum(piece * normed, axis=0), jnp.sum(piece, axis=0)])
    for name in ("tp", "fsdp", "rep"):
        col_sums = butterfly_sum(col_sums, name, sizes[name])
    whole_gain, whole_bias = col_sums[0], col_sums[1]
    grad_gain = lax.dynamic_slice_in_dim(whole_gain, col_start, own_width, 0)
    grad_bias = lax.dynamic_slice_in_dim(whole_bias, col_start, own_width, 0)
    term_in = contract_rows(scaled, back_hidden).astype(jnp.bfloat16)
    term_out = contract_rows(active, chosen).astype(jnp.bfloat16)
    shard_in = pair_scatter(term_in, 0)
    shard_out = pair_scatter(term_out, 1)
    both = jnp.concatenate([shard_in.reshape(-1), shard_out.reshape(-1)])
    both, branch = lax.optimization_barrier((both, branch))
    block_out = (tokens.astype(jnp.float32) + branch).astype(jnp.bfloat16)
    total = ring_allreduce(both, "rep", sizes["rep"])
    total, back_normed = lax.optimization_barrier((total, back_normed))
    shard_in = total[: shard_in.size].reshape(shard_in.shape)
    shard_out = total[shard_in.size :].reshape(shard_out.shape)
    normed_own = lax.dynamic_slice_in_dim(normed, col_start, own_width, 1)
    gain_own = ln_gain.astype(jnp.float32)
    back_scaled = back_normed * gain_own
    mean_plain = (sum_plain / width)[:, None]
    mean_cross = (sum_cross / width)[:, None]
    back_rows = inv_std * (back_scaled - mean_plain - normed_own * mean_cross)
    input_grad = (chosen_own.astype(jnp.float32) + back_rows).astype(jnp.bfloat16)
    grad_in = apply_blocks(shard_in, blocks_in, jnp.float32)
    grad_out = apply_blocks(shard_out, blocks_out, jnp.float32)
    return (block_out, input_grad, grad_in, grad_out, grad_gain, grad_bias)


def solution(mesh):
    placed = (
        P(("rep", "fsdp"), "tp"),
        P(("rep", "fsdp"), "tp"),
        P(("rep", "fsdp")),
        P("tp"),
        P("tp"),
        P("fsdp", "tp"),
        P("tp", "fsdp"),
        P("fsdp", "tp"),
        P("tp", "fsdp"),
    )
    return jax.shard_map(
        partial(on_device, dict(mesh.shape)),
        mesh=mesh,
        in_specs=placed,
        out_specs=(
            P(("rep", "fsdp"), "tp"),
            P(("rep", "fsdp"), "tp"),
            P("fsdp", "tp"),
            P("tp", "fsdp"),
            P("tp"),
            P("tp"),
        ),
        check_vma=False,
    )
```

```python
from functools import partial

import jax
import jax.numpy as jnp
from jax import lax
from jax.sharding import PartitionSpec as P

BLK = 128


def apply_blocks(weight, blocks, kind):
    row_blocks, col_blocks = blocks.shape
    shaped = weight.reshape(row_blocks, BLK, col_blocks, BLK)
    keeper = blocks.astype(kind)[:, None, :, None]
    return (shaped * keeper).reshape(weight.shape)


def contract_rows(left, right):
    return lax.dot_general(
        left, right, (((0,), (0,)), ((), ())), preferred_element_type=jnp.float32
    )


def contract_cols(left, right):
    return lax.dot_general(
        left, right, (((1,), (1,)), ((), ())), preferred_element_type=jnp.float32
    )


def pair_gather(own, axis):
    other = lax.ppermute(own, "fsdp", perm=[(0, 1), (1, 0)])
    first = lax.axis_index("fsdp") == 0
    low = jnp.where(first, own, other)
    high = jnp.where(first, other, own)
    return jnp.concatenate([low, high], axis=axis)


def pair_scatter(term, axis):
    half = term.shape[axis] // 2
    idx = lax.axis_index("fsdp")
    keep = lax.dynamic_slice_in_dim(term, idx * half, half, axis)
    send = lax.dynamic_slice_in_dim(term, (1 - idx) * half, half, axis)
    recv = lax.ppermute(send, "fsdp", perm=[(0, 1), (1, 0)])
    return keep.astype(jnp.float32) + recv.astype(jnp.float32)


def ring_allreduce(flat, axis, size):
    me = lax.axis_index(axis)
    halves = flat.reshape(2, size, -1)
    fwd = [(i, (i + 1) % size) for i in range(size)]
    bwd = [(i, (i - 1) % size) for i in range(size)]
    parts = []
    for direction, perm in ((1, fwd), (-1, bwd)):
        chunks = halves[0 if direction == 1 else 1]
        acc = lax.dynamic_index_in_dim(chunks, me % size, 0, keepdims=False)
        for step in range(size - 1):
            recv = lax.ppermute(acc.astype(jnp.bfloat16), axis, perm=perm)
            src = (me - direction * (step + 1)) % size
            acc = recv.astype(jnp.float32) + lax.dynamic_index_in_dim(
                chunks, src, 0, keepdims=False
            )
        owned = (me - direction * (size - 1)) % size
        pieces = [acc.astype(jnp.bfloat16)]
        for step in range(size - 1):
            pieces.append(lax.ppermute(pieces[-1], axis, perm=perm))
        values = [lax.reduce_precision(acc, exponent_bits=8, mantissa_bits=7)]
        values += [p.astype(jnp.float32) for p in pieces[1:]]
        slots = []
        for slot in range(size):
            pick = (direction * (owned - slot)) % size
            value = values[0]
            for j in range(1, size):
                value = jnp.where(pick == j, values[j], value)
            slots.append(value)
        parts.append(jnp.stack(slots))
    return jnp.stack(parts).reshape(flat.shape)


def butterfly_sum(values, axis, size):
    bit = 1
    while bit < size:
        perm = [(i, i ^ bit) for i in range(size)]
        values = values + lax.ppermute(values, axis, perm=perm)
        bit *= 2
    return values


def on_device(
    sizes,
    tokens, cotangent, frame_mask, ln_gain, ln_bias, weight_in, weight_out, blocks_in, blocks_out
):
    frames = tokens.shape[0]
    stacked = jnp.concatenate(
        [tokens, ln_gain[None], ln_bias[None], jnp.zeros((6, tokens.shape[1]), tokens.dtype)]
    )
    gathered = lax.all_to_all(
        jnp.tile(stacked, (1, sizes["tp"])), "tp", split_axis=1, concat_axis=1, tiled=True
    )
    whole_rows = gathered[:frames]
    gain_full, bias_full = gathered[frames], gathered[frames + 1]
    masked_in = apply_blocks(weight_in, blocks_in, jnp.bfloat16)
    masked_out = apply_blocks(weight_out, blocks_out, jnp.bfloat16)
    full_in = pair_gather(masked_in, 0)
    full_out = pair_gather(masked_out, 1)
    width = whole_rows.shape[1]
    own_width = tokens.shape[1]
    col_start = lax.axis_index("tp") * own_width
    gelu_exact = partial(jax.nn.gelu, approximate=False)
    values = whole_rows.astype(jnp.float32)
    centre = jnp.mean(values, axis=1, keepdims=True)
    centred = values - centre
    inv_std = lax.rsqrt(jnp.mean(centred * centred, axis=1, keepdims=True) + 1e-05)
    normed = centred * inv_std
    gain_f = gain_full.astype(jnp.float32)
    scaled = (normed * gain_f + bias_full.astype(jnp.float32)).astype(jnp.bfloat16)
    hidden = jnp.dot(scaled, full_in, preferred_element_type=jnp.float32)
    active = gelu_exact(hidden).astype(jnp.bfloat16)
    partial_out = jnp.dot(active, full_out, preferred_element_type=jnp.float32)
    partial_out = partial_out.astype(jnp.bfloat16)
    whole_grad = lax.all_gather(cotangent, "tp", axis=1, tiled=True)
    unused, whole_grad = lax.optimization_barrier((partial_out, whole_grad))
    branch = lax.psum_scatter(
        partial_out, "tp", scatter_dimension=1, tiled=True
    ).astype(jnp.float32)
    flags = frame_mask[:, None].astype(jnp.bfloat16)
    chosen = whole_grad * flags
    chosen_own = cotangent * flags
    back_active = contract_cols(chosen, full_out)
    unused, gelu_back = jax.vjp(gelu_exact, hidden)
    back_hidden = gelu_back(back_active)[0].astype(jnp.bfloat16)
    partial_normed = contract_cols(back_hidden, full_in).astype(jnp.bfloat16)
    received = lax.all_to_all(partial_normed, "tp", split_axis=1, concat_axis=0, tiled=True)
    back_normed = jnp.sum(
        received.reshape(sizes["tp"], frames, -1).astype(jnp.float32), axis=0
    )
    piece = partial_normed.astype(jnp.float32)
    piece_scaled = piece * gain_f
    row_sums = butterfly_sum(
        jnp.stack([jnp.sum(piece_scaled, axis=1), jnp.sum(piece_scaled * normed, axis=1)]),
        "tp",
        sizes["tp"],
    )
    sum_plain, sum_cross = row_sums[0], row_sums[1]
    col_sums = jnp.stack([jnp.sum(piece * normed, axis=0), jnp.sum(piece, axis=0)])
    for name in ("tp", "fsdp", "rep"):
        col_sums = butterfly_sum(col_sums, name, sizes[name])
    whole_gain, whole_bias = col_sums[0], col_sums[1]
    grad_gain = lax.dynamic_slice_in_dim(whole_gain, col_start, own_width, 0)
    grad_bias = lax.dynamic_slice_in_dim(whole_bias, col_start, own_width, 0)
    term_in = contract_rows(scaled, back_hidden).astype(jnp.bfloat16)
    term_out = contract_rows(active, chosen).astype(jnp.bfloat16)
    shard_in = pair_scatter(term_in, 0)
    shard_out = pair_scatter(term_out, 1)
    both = jnp.concatenate([shard_in.reshape(-1), shard_out.reshape(-1)])
    both, branch = lax.optimization_barrier((both, branch))
    block_out = (tokens.astype(jnp.float32) + branch).astype(jnp.bfloat16)
    total = ring_allreduce(both, "rep", sizes["rep"])
    total, back_normed = lax.optimization_barrier((total, back_normed))
    shard_in = total[: shard_in.size].reshape(shard_in.shape)
    shard_out = total[shard_in.size :].reshape(shard_out.shape)
    normed_own = lax.dynamic_slice_in_dim(normed, col_start, own_width, 1)
    gain_own = ln_gain.astype(jnp.float32)
    back_scaled = back_normed * gain_own
    mean_plain = (sum_plain / width)[:, None]
    mean_cross = (sum_cross / width)[:, None]
    back_rows = inv_std * (back_scaled - mean_plain - normed_own * mean_cross)
    input_grad = (chosen_own.astype(jnp.float32) + back_rows).astype(jnp.bfloat16)
    grad_in = apply_blocks(shard_in, blocks_in, jnp.float32)
    grad_out = apply_blocks(shard_out, blocks_out, jnp.float32)
    return (block_out, input_grad, grad_in, grad_out, grad_gain, grad_bias)


def solution(mesh):
    placed = (
        P(("rep", "fsdp"), "tp"),
        P(("rep", "fsdp"), "tp"),
        P(("rep", "fsdp")),
        P("tp"),
        P("tp"),
        P("fsdp", "tp"),
        P("tp", "fsdp"),
        P("fsdp", "tp"),
        P("tp", "fsdp"),
    )
    return jax.shard_map(
        partial(on_device, dict(mesh.shape)),
        mesh=mesh,
        in_specs=placed,
        out_specs=(
            P(("rep", "fsdp"), "tp"),
            P(("rep", "fsdp"), "tp"),
            P("fsdp", "tp"),
            P("tp", "fsdp"),
            P("tp"),
            P("tp"),
        ),
        check_vma=False,
    )
```

```python
from functools import partial

import jax
import jax.numpy as jnp
from jax import lax
from jax.sharding import PartitionSpec as P

BLK = 128


def apply_blocks(weight, blocks, kind):
    row_blocks, col_blocks = blocks.shape
    shaped = weight.reshape(row_blocks, BLK, col_blocks, BLK)
    keeper = blocks.astype(kind)[:, None, :, None]
    return (shaped * keeper).reshape(weight.shape)


def contract_rows(left, right):
    return lax.dot_general(
        left, right, (((0,), (0,)), ((), ())), preferred_element_type=jnp.float32
    )


def contract_cols(left, right):
    return lax.dot_general(
        left, right, (((1,), (1,)), ((), ())), preferred_element_type=jnp.float32
    )


def pair_gather(own, axis):
    other = lax.ppermute(own, "fsdp", perm=[(0, 1), (1, 0)])
    first = lax.axis_index("fsdp") == 0
    low = jnp.where(first, own, other)
    high = jnp.where(first, other, own)
    return jnp.concatenate([low, high], axis=axis)


def pair_scatter(term, axis):
    half = term.shape[axis] // 2
    idx = lax.axis_index("fsdp")
    keep = lax.dynamic_slice_in_dim(term, idx * half, half, axis)
    send = lax.dynamic_slice_in_dim(term, (1 - idx) * half, half, axis)
    recv = lax.ppermute(send, "fsdp", perm=[(0, 1), (1, 0)])
    return keep.astype(jnp.float32) + recv.astype(jnp.float32)


def ring_allreduce(flat, axis, size):
    me = lax.axis_index(axis)
    halves = flat.reshape(2, size, -1)
    fwd = [(i, (i + 1) % size) for i in range(size)]
    bwd = [(i, (i - 1) % size) for i in range(size)]
    parts = []
    for direction, perm in ((1, fwd), (-1, bwd)):
        chunks = halves[0 if direction == 1 else 1]
        acc = lax.dynamic_index_in_dim(chunks, me % size, 0, keepdims=False)
        for step in range(size - 1):
            recv = lax.ppermute(acc.astype(jnp.bfloat16), axis, perm=perm)
            src = (me - direction * (step + 1)) % size
            acc = recv.astype(jnp.float32) + lax.dynamic_index_in_dim(
                chunks, src, 0, keepdims=False
            )
        owned = (me - direction * (size - 1)) % size
        pieces = [acc.astype(jnp.bfloat16)]
        for step in range(size - 1):
            pieces.append(lax.ppermute(pieces[-1], axis, perm=perm))
        values = [lax.reduce_precision(acc, exponent_bits=8, mantissa_bits=7)]
        values += [p.astype(jnp.float32) for p in pieces[1:]]
        slots = []
        for slot in range(size):
            pick = (direction * (owned - slot)) % size
            value = values[0]
            for j in range(1, size):
                value = jnp.where(pick == j, values[j], value)
            slots.append(value)
        parts.append(jnp.stack(slots))
    return jnp.stack(parts).reshape(flat.shape)


def butterfly_sum(values, axis, size):
    bit = 1
    while bit < size:
        perm = [(i, i ^ bit) for i in range(size)]
        values = values + lax.ppermute(values, axis, perm=perm)
        bit *= 2
    return values


def on_device(
    sizes,
    tokens, cotangent, frame_mask, ln_gain, ln_bias, weight_in, weight_out, blocks_in, blocks_out
):
    frames = tokens.shape[0]
    stacked = jnp.concatenate(
        [tokens, ln_gain[None], ln_bias[None], jnp.zeros((6, tokens.shape[1]), tokens.dtype)]
    )
    gathered = lax.all_to_all(
        jnp.tile(stacked, (1, sizes["tp"])), "tp", split_axis=1, concat_axis=1, tiled=True
    )
    whole_rows = gathered[:frames]
    gain_full, bias_full = gathered[frames], gathered[frames + 1]
    masked_in = apply_blocks(weight_in, blocks_in, jnp.bfloat16)
    masked_out = apply_blocks(weight_out, blocks_out, jnp.bfloat16)
    full_in = pair_gather(masked_in, 0)
    full_out = pair_gather(masked_out, 1)
    width = whole_rows.shape[1]
    own_width = tokens.shape[1]
    col_start = lax.axis_index("tp") * own_width
    gelu_exact = partial(jax.nn.gelu, approximate=False)
    values = whole_rows.astype(jnp.float32)
    centre = jnp.mean(values, axis=1, keepdims=True)
    centred = values - centre
    inv_std = lax.rsqrt(jnp.mean(centred * centred, axis=1, keepdims=True) + 1e-05)
    normed = centred * inv_std
    gain_f = gain_full.astype(jnp.float32)
    scaled = (normed * gain_f + bias_full.astype(jnp.float32)).astype(jnp.bfloat16)
    hidden = jnp.dot(scaled, full_in, preferred_element_type=jnp.float32)
    active = gelu_exact(hidden).astype(jnp.bfloat16)
    partial_out = lax.dot_general(
        full_out, active, (((0,), (1,)), ((), ())), preferred_element_type=jnp.float32
    ).astype(jnp.bfloat16)
    whole_grad = lax.all_gather(cotangent, "tp", axis=1, tiled=True)
    unused, whole_grad = lax.optimization_barrier((partial_out, whole_grad))
    branch = lax.psum_scatter(
        partial_out, "tp", scatter_dimension=0, tiled=True
    ).astype(jnp.float32).T
    flags = frame_mask[:, None].astype(jnp.bfloat16)
    chosen = whole_grad * flags
    chosen_own = cotangent * flags
    back_active = contract_cols(chosen, full_out)
    unused, gelu_back = jax.vjp(gelu_exact, hidden)
    back_hidden = gelu_back(back_active)[0].astype(jnp.bfloat16)
    partial_normed = contract_cols(back_hidden, full_in).astype(jnp.bfloat16)
    back_normed = lax.psum_scatter(
        partial_normed, "tp", scatter_dimension=1, tiled=True
    ).astype(jnp.float32)
    piece = partial_normed.astype(jnp.float32)
    piece_scaled = piece * gain_f
    row_sums = butterfly_sum(
        jnp.stack([jnp.sum(piece_scaled, axis=1), jnp.sum(piece_scaled * normed, axis=1)]),
        "tp",
        sizes["tp"],
    )
    sum_plain, sum_cross = row_sums[0], row_sums[1]
    col_sums = jnp.stack([jnp.sum(piece * normed, axis=0), jnp.sum(piece, axis=0)])
    for name in ("tp", "fsdp", "rep"):
        col_sums = butterfly_sum(col_sums, name, sizes[name])
    whole_gain, whole_bias = col_sums[0], col_sums[1]
    grad_gain = lax.dynamic_slice_in_dim(whole_gain, col_start, own_width, 0)
    grad_bias = lax.dynamic_slice_in_dim(whole_bias, col_start, own_width, 0)
    term_in = contract_rows(scaled, back_hidden).astype(jnp.bfloat16)
    term_out = contract_rows(active, chosen).astype(jnp.bfloat16)
    shard_in = pair_scatter(term_in, 0)
    shard_out = pair_scatter(term_out, 1)
    both = jnp.concatenate([shard_in.reshape(-1), shard_out.reshape(-1)])
    both, branch = lax.optimization_barrier((both, branch))
    block_out = (tokens.astype(jnp.float32) + branch).astype(jnp.bfloat16)
    total = ring_allreduce(both, "rep", sizes["rep"])
    total, back_normed = lax.optimization_barrier((total, back_normed))
    shard_in = total[: shard_in.size].reshape(shard_in.shape)
    shard_out = total[shard_in.size :].reshape(shard_out.shape)
    normed_own = lax.dynamic_slice_in_dim(normed, col_start, own_width, 1)
    gain_own = ln_gain.astype(jnp.float32)
    back_scaled = back_normed * gain_own
    mean_plain = (sum_plain / width)[:, None]
    mean_cross = (sum_cross / width)[:, None]
    back_rows = inv_std * (back_scaled - mean_plain - normed_own * mean_cross)
    input_grad = (chosen_own.astype(jnp.float32) + back_rows).astype(jnp.bfloat16)
    grad_in = apply_blocks(shard_in, blocks_in, jnp.float32)
    grad_out = apply_blocks(shard_out, blocks_out, jnp.float32)
    return (block_out, input_grad, grad_in, grad_out, grad_gain, grad_bias)


def solution(mesh):
    placed = (
        P(("rep", "fsdp"), "tp"),
        P(("rep", "fsdp"), "tp"),
        P(("rep", "fsdp")),
        P("tp"),
        P("tp"),
        P("fsdp", "tp"),
        P("tp", "fsdp"),
        P("fsdp", "tp"),
        P("tp", "fsdp"),
    )
    return jax.shard_map(
        partial(on_device, dict(mesh.shape)),
        mesh=mesh,
        in_specs=placed,
        out_specs=(
            P(("rep", "fsdp"), "tp"),
            P(("rep", "fsdp"), "tp"),
            P("fsdp", "tp"),
            P("tp", "fsdp"),
            P("tp"),
            P("tp"),
        ),
        check_vma=False,
    )
```

```python
from functools import partial

import jax
import jax.numpy as jnp
from jax import lax
from jax.sharding import PartitionSpec as P

BLK = 128


def apply_blocks(weight, blocks, kind):
    row_blocks, col_blocks = blocks.shape
    shaped = weight.reshape(row_blocks, BLK, col_blocks, BLK)
    keeper = blocks.astype(kind)[:, None, :, None]
    return (shaped * keeper).reshape(weight.shape)


def contract_rows(left, right):
    return lax.dot_general(
        left, right, (((0,), (0,)), ((), ())), preferred_element_type=jnp.float32
    )


def contract_cols(left, right):
    return lax.dot_general(
        left, right, (((1,), (1,)), ((), ())), preferred_element_type=jnp.float32
    )


def pair_gather(own, axis):
    other = lax.ppermute(own, "fsdp", perm=[(0, 1), (1, 0)])
    first = lax.axis_index("fsdp") == 0
    low = jnp.where(first, own, other)
    high = jnp.where(first, other, own)
    return jnp.concatenate([low, high], axis=axis)


def pair_scatter(term, axis):
    half = term.shape[axis] // 2
    idx = lax.axis_index("fsdp")
    keep = lax.dynamic_slice_in_dim(term, idx * half, half, axis)
    send = lax.dynamic_slice_in_dim(term, (1 - idx) * half, half, axis)
    recv = lax.ppermute(send, "fsdp", perm=[(0, 1), (1, 0)])
    return keep.astype(jnp.float32) + recv.astype(jnp.float32)


def ring_allreduce(flat, axis, size):
    me = lax.axis_index(axis)
    halves = flat.reshape(2, size, -1)
    fwd = [(i, (i + 1) % size) for i in range(size)]
    bwd = [(i, (i - 1) % size) for i in range(size)]
    parts = []
    for direction, perm in ((1, fwd), (-1, bwd)):
        chunks = halves[0 if direction == 1 else 1]
        acc = lax.dynamic_index_in_dim(chunks, me % size, 0, keepdims=False)
        for step in range(size - 1):
            recv = lax.ppermute(acc.astype(jnp.bfloat16), axis, perm=perm)
            src = (me - direction * (step + 1)) % size
            acc = recv.astype(jnp.float32) + lax.dynamic_index_in_dim(
                chunks, src, 0, keepdims=False
            )
        owned = (me - direction * (size - 1)) % size
        pieces = [acc.astype(jnp.bfloat16)]
        for step in range(size - 1):
            pieces.append(lax.ppermute(pieces[-1], axis, perm=perm))
        values = [lax.reduce_precision(acc, exponent_bits=8, mantissa_bits=7)]
        values += [p.astype(jnp.float32) for p in pieces[1:]]
        slots = []
        for slot in range(size):
            pick = (direction * (owned - slot)) % size
            value = values[0]
            for j in range(1, size):
                value = jnp.where(pick == j, values[j], value)
            slots.append(value)
        parts.append(jnp.stack(slots))
    return jnp.stack(parts).reshape(flat.shape)


def butterfly_sum(values, axis, size):
    bit = 1
    while bit < size:
        perm = [(i, i ^ bit) for i in range(size)]
        values = values + lax.ppermute(values, axis, perm=perm)
        bit *= 2
    return values


def on_device(
    sizes,
    tokens, cotangent, frame_mask, ln_gain, ln_bias, weight_in, weight_out, blocks_in, blocks_out
):
    frames = tokens.shape[0]
    stacked = jnp.concatenate(
        [tokens, ln_gain[None], ln_bias[None], jnp.zeros((6, tokens.shape[1]), tokens.dtype)]
    )
    gathered = lax.all_to_all(
        jnp.tile(stacked, (1, sizes["tp"])), "tp", split_axis=1, concat_axis=1, tiled=True
    )
    whole_rows = gathered[:frames]
    gain_full, bias_full = gathered[frames], gathered[frames + 1]
    masked_in = apply_blocks(weight_in, blocks_in, jnp.bfloat16)
    masked_out = apply_blocks(weight_out, blocks_out, jnp.bfloat16)
    full_in = pair_gather(masked_in, 0)
    full_out = pair_gather(masked_out, 1)
    width = whole_rows.shape[1]
    own_width = tokens.shape[1]
    col_start = lax.axis_index("tp") * own_width
    gelu_exact = partial(jax.nn.gelu, approximate=False)
    values = whole_rows.astype(jnp.float32)
    centre = jnp.mean(values, axis=1, keepdims=True)
    centred = values - centre
    inv_std = lax.rsqrt(jnp.mean(centred * centred, axis=1, keepdims=True) + 1e-05)
    normed = centred * inv_std
    gain_f = gain_full.astype(jnp.float32)
    scaled = (normed * gain_f + bias_full.astype(jnp.float32)).astype(jnp.bfloat16)
    hidden = jnp.dot(scaled, full_in, preferred_element_type=jnp.float32)
    active = gelu_exact(hidden).astype(jnp.bfloat16)
    partial_out = lax.dot_general(
        full_out, active, (((0,), (1,)), ((), ())), preferred_element_type=jnp.float32
    ).astype(jnp.bfloat16)
    whole_grad = lax.all_gather(cotangent, "tp", axis=1, tiled=True)
    unused, whole_grad = lax.optimization_barrier((partial_out, whole_grad))
    branch = lax.psum_scatter(
        partial_out, "tp", scatter_dimension=0, tiled=True
    ).astype(jnp.float32).T
    flags = frame_mask[:, None].astype(jnp.bfloat16)
    chosen = whole_grad * flags
    chosen_own = cotangent * flags
    back_active = contract_cols(chosen, full_out)
    unused, gelu_back = jax.vjp(gelu_exact, hidden)
    back_hidden = gelu_back(back_active)[0].astype(jnp.bfloat16)
    partial_normed = contract_cols(back_hidden, full_in).astype(jnp.bfloat16)
    back_normed = lax.psum_scatter(
        partial_normed, "tp", scatter_dimension=1, tiled=True
    ).astype(jnp.float32)
    piece = partial_normed.astype(jnp.float32)
    piece_scaled = piece * gain_f
    row_sums = butterfly_sum(
        jnp.stack([jnp.sum(piece_scaled, axis=1), jnp.sum(piece_scaled * normed, axis=1)]),
        "tp",
        sizes["tp"],
    )
    sum_plain, sum_cross = row_sums[0], row_sums[1]
    col_sums = jnp.stack([jnp.sum(piece * normed, axis=0), jnp.sum(piece, axis=0)])
    for name in ("tp", "fsdp", "rep"):
        col_sums = butterfly_sum(col_sums, name, sizes[name])
    whole_gain, whole_bias = col_sums[0], col_sums[1]
    grad_gain = lax.dynamic_slice_in_dim(whole_gain, col_start, own_width, 0)
    grad_bias = lax.dynamic_slice_in_dim(whole_bias, col_start, own_width, 0)
    term_in = contract_rows(scaled, back_hidden).astype(jnp.bfloat16)
    term_out = contract_rows(active, chosen).astype(jnp.bfloat16)
    shard_in = pair_scatter(term_in, 0)
    shard_out = pair_scatter(term_out, 1)
    both = jnp.concatenate([shard_in.reshape(-1), shard_out.reshape(-1)])
    both, branch = lax.optimization_barrier((both, branch))
    block_out = (tokens.astype(jnp.float32) + branch).astype(jnp.bfloat16)
    total = ring_allreduce(both, "rep", sizes["rep"])
    shard_in = total[: shard_in.size].reshape(shard_in.shape)
    shard_out = total[shard_in.size :].reshape(shard_out.shape)
    grad_in = apply_blocks(shard_in, blocks_in, jnp.float32)
    grad_out = apply_blocks(shard_out, blocks_out, jnp.float32)
    grad_in, grad_out, back_normed = lax.optimization_barrier((grad_in, grad_out, back_normed))
    normed_own = lax.dynamic_slice_in_dim(normed, col_start, own_width, 1)
    gain_own = ln_gain.astype(jnp.float32)
    back_scaled = back_normed * gain_own
    mean_plain = (sum_plain / width)[:, None]
    mean_cross = (sum_cross / width)[:, None]
    back_rows = inv_std * (back_scaled - mean_plain - normed_own * mean_cross)
    input_grad = (chosen_own.astype(jnp.float32) + back_rows).astype(jnp.bfloat16)
    return (block_out, input_grad, grad_in, grad_out, grad_gain, grad_bias)


def solution(mesh):
    placed = (
        P(("rep", "fsdp"), "tp"),
        P(("rep", "fsdp"), "tp"),
        P(("rep", "fsdp")),
        P("tp"),
        P("tp"),
        P("fsdp", "tp"),
        P("tp", "fsdp"),
        P("fsdp", "tp"),
        P("tp", "fsdp"),
    )
    return jax.shard_map(
        partial(on_device, dict(mesh.shape)),
        mesh=mesh,
        in_specs=placed,
        out_specs=(
            P(("rep", "fsdp"), "tp"),
            P(("rep", "fsdp"), "tp"),
            P("fsdp", "tp"),
            P("tp", "fsdp"),
            P("tp"),
            P("tp"),
        ),
        check_vma=False,
    )
```

```python
from functools import partial

import jax
import jax.numpy as jnp
from jax import lax
from jax.sharding import PartitionSpec as P

BLK = 128


def apply_blocks(weight, blocks, kind):
    row_blocks, col_blocks = blocks.shape
    shaped = weight.reshape(row_blocks, BLK, col_blocks, BLK)
    keeper = blocks.astype(kind)[:, None, :, None]
    return (shaped * keeper).reshape(weight.shape)


def contract_rows(left, right):
    return lax.dot_general(
        left, right, (((0,), (0,)), ((), ())), preferred_element_type=jnp.float32
    )


def contract_cols(left, right):
    return lax.dot_general(
        left, right, (((1,), (1,)), ((), ())), preferred_element_type=jnp.float32
    )


def pair_gather(own, axis):
    other = lax.ppermute(own, "fsdp", perm=[(0, 1), (1, 0)])
    first = lax.axis_index("fsdp") == 0
    low = jnp.where(first, own, other)
    high = jnp.where(first, other, own)
    return jnp.concatenate([low, high], axis=axis)


def pair_scatter(term, axis):
    half = term.shape[axis] // 2
    idx = lax.axis_index("fsdp")
    keep = lax.dynamic_slice_in_dim(term, idx * half, half, axis)
    send = lax.dynamic_slice_in_dim(term, (1 - idx) * half, half, axis)
    recv = lax.ppermute(send, "fsdp", perm=[(0, 1), (1, 0)])
    return keep.astype(jnp.float32) + recv.astype(jnp.float32)


def ring_allreduce(flat, axis, size):
    me = lax.axis_index(axis)
    halves = flat.reshape(2, size, -1)
    fwd = [(i, (i + 1) % size) for i in range(size)]
    bwd = [(i, (i - 1) % size) for i in range(size)]
    parts = []
    for direction, perm in ((1, fwd), (-1, bwd)):
        chunks = halves[0 if direction == 1 else 1]
        acc = lax.dynamic_index_in_dim(chunks, me % size, 0, keepdims=False)
        for step in range(size - 1):
            recv = lax.ppermute(acc.astype(jnp.bfloat16), axis, perm=perm)
            src = (me - direction * (step + 1)) % size
            acc = recv.astype(jnp.float32) + lax.dynamic_index_in_dim(
                chunks, src, 0, keepdims=False
            )
        owned = (me - direction * (size - 1)) % size
        pieces = [acc.astype(jnp.bfloat16)]
        for step in range(size - 1):
            pieces.append(lax.ppermute(pieces[-1], axis, perm=perm))
        values = [lax.reduce_precision(acc, exponent_bits=8, mantissa_bits=7)]
        values += [p.astype(jnp.float32) for p in pieces[1:]]
        slots = []
        for slot in range(size):
            pick = (direction * (owned - slot)) % size
            value = values[0]
            for j in range(1, size):
                value = jnp.where(pick == j, values[j], value)
            slots.append(value)
        parts.append(jnp.stack(slots))
    return jnp.stack(parts).reshape(flat.shape)


def butterfly_sum(values, axis, size):
    bit = 1
    while bit < size:
        perm = [(i, i ^ bit) for i in range(size)]
        values = values + lax.ppermute(values, axis, perm=perm)
        bit *= 2
    return values


def on_device(
    sizes,
    tokens, cotangent, frame_mask, ln_gain, ln_bias, weight_in, weight_out, blocks_in, blocks_out
):
    frames = tokens.shape[0]
    stacked = jnp.concatenate(
        [tokens, ln_gain[None], ln_bias[None], jnp.zeros((6, tokens.shape[1]), tokens.dtype)]
    )
    gathered = lax.all_to_all(
        jnp.tile(stacked, (1, sizes["tp"])), "tp", split_axis=1, concat_axis=1, tiled=True
    )
    whole_rows = gathered[:frames]
    gain_full, bias_full = gathered[frames], gathered[frames + 1]
    masked_in = apply_blocks(weight_in, blocks_in, jnp.bfloat16)
    masked_out = apply_blocks(weight_out, blocks_out, jnp.bfloat16)
    full_in = pair_gather(masked_in, 0)
    full_out = pair_gather(masked_out, 1)
    width = whole_rows.shape[1]
    own_width = tokens.shape[1]
    col_start = lax.axis_index("tp") * own_width
    gelu_exact = partial(jax.nn.gelu, approximate=False)
    values = whole_rows.astype(jnp.float32)
    centre = jnp.mean(values, axis=1, keepdims=True)
    centred = values - centre
    inv_std = lax.rsqrt(jnp.mean(centred * centred, axis=1, keepdims=True) + 1e-05)
    normed = centred * inv_std
    gain_f = gain_full.astype(jnp.float32)
    scaled = (normed * gain_f + bias_full.astype(jnp.float32)).astype(jnp.bfloat16)
    hidden = jnp.dot(scaled, full_in, preferred_element_type=jnp.float32)
    active = gelu_exact(hidden).astype(jnp.bfloat16)
    partial_out = lax.dot_general(
        full_out, active, (((0,), (1,)), ((), ())), preferred_element_type=jnp.float32
    ).astype(jnp.bfloat16)
    whole_grad = lax.all_gather(cotangent, "tp", axis=1, tiled=True)
    unused, whole_grad = lax.optimization_barrier((partial_out, whole_grad))
    branch = lax.psum_scatter(
        partial_out, "tp", scatter_dimension=0, tiled=True
    ).astype(jnp.float32).T
    flags = frame_mask[:, None].astype(jnp.bfloat16)
    chosen = whole_grad * flags
    chosen_own = cotangent * flags
    back_active = contract_cols(chosen, full_out)
    unused, gelu_back = jax.vjp(gelu_exact, hidden)
    back_hidden = gelu_back(back_active)[0].astype(jnp.bfloat16)
    partial_normed = contract_cols(back_hidden, full_in).astype(jnp.bfloat16)
    back_normed = lax.psum_scatter(
        partial_normed, "tp", scatter_dimension=1, tiled=True
    ).astype(jnp.float32)
    piece = partial_normed.astype(jnp.float32)
    piece_scaled = piece * gain_f
    row_sums = jnp.stack([jnp.sum(piece_scaled, axis=1), jnp.sum(piece_scaled * normed, axis=1)])
    col_sums = jnp.stack([jnp.sum(piece * normed, axis=0), jnp.sum(piece, axis=0)])
    both_sums = butterfly_sum(jnp.concatenate([row_sums, col_sums], axis=1), "tp", sizes["tp"])
    row_sums, col_sums = both_sums[:, :frames], both_sums[:, frames:]
    sum_plain, sum_cross = row_sums[0], row_sums[1]
    for name in ("fsdp", "rep"):
        col_sums = butterfly_sum(col_sums, name, sizes[name])
    whole_gain, whole_bias = col_sums[0], col_sums[1]
    grad_gain = lax.dynamic_slice_in_dim(whole_gain, col_start, own_width, 0)
    grad_bias = lax.dynamic_slice_in_dim(whole_bias, col_start, own_width, 0)
    term_in = contract_rows(scaled, back_hidden).astype(jnp.bfloat16)
    term_out = contract_rows(active, chosen).astype(jnp.bfloat16)
    shard_in = pair_scatter(term_in, 0)
    shard_out = pair_scatter(term_out, 1)
    both = jnp.concatenate([shard_in.reshape(-1), shard_out.reshape(-1)])
    both, branch = lax.optimization_barrier((both, branch))
    block_out = (tokens.astype(jnp.float32) + branch).astype(jnp.bfloat16)
    total = ring_allreduce(both, "rep", sizes["rep"])
    shard_in = total[: shard_in.size].reshape(shard_in.shape)
    shard_out = total[shard_in.size :].reshape(shard_out.shape)
    grad_in = apply_blocks(shard_in, blocks_in, jnp.float32)
    grad_out = apply_blocks(shard_out, blocks_out, jnp.float32)
    grad_in, grad_out, back_normed = lax.optimization_barrier((grad_in, grad_out, back_normed))
    normed_own = lax.dynamic_slice_in_dim(normed, col_start, own_width, 1)
    gain_own = ln_gain.astype(jnp.float32)
    back_scaled = back_normed * gain_own
    mean_plain = (sum_plain / width)[:, None]
    mean_cross = (sum_cross / width)[:, None]
    back_rows = inv_std * (back_scaled - mean_plain - normed_own * mean_cross)
    input_grad = (chosen_own.astype(jnp.float32) + back_rows).astype(jnp.bfloat16)
    return (block_out, input_grad, grad_in, grad_out, grad_gain, grad_bias)


def solution(mesh):
    placed = (
        P(("rep", "fsdp"), "tp"),
        P(("rep", "fsdp"), "tp"),
        P(("rep", "fsdp")),
        P("tp"),
        P("tp"),
        P("fsdp", "tp"),
        P("tp", "fsdp"),
        P("fsdp", "tp"),
        P("tp", "fsdp"),
    )
    return jax.shard_map(
        partial(on_device, dict(mesh.shape)),
        mesh=mesh,
        in_specs=placed,
        out_specs=(
            P(("rep", "fsdp"), "tp"),
            P(("rep", "fsdp"), "tp"),
            P("fsdp", "tp"),
            P("tp", "fsdp"),
            P("tp"),
            P("tp"),
        ),
        check_vma=False,
    )
```

```python
from functools import partial

import jax
import jax.numpy as jnp
from jax import lax
from jax.sharding import PartitionSpec as P

BLK = 128


def apply_blocks(weight, blocks, kind):
    row_blocks, col_blocks = blocks.shape
    shaped = weight.reshape(row_blocks, BLK, col_blocks, BLK)
    keeper = blocks.astype(kind)[:, None, :, None]
    return (shaped * keeper).reshape(weight.shape)


def contract_rows(left, right):
    return lax.dot_general(
        left, right, (((0,), (0,)), ((), ())), preferred_element_type=jnp.float32
    )


def contract_cols(left, right):
    return lax.dot_general(
        left, right, (((1,), (1,)), ((), ())), preferred_element_type=jnp.float32
    )


def pair_gather(own, axis):
    other = lax.ppermute(own, "fsdp", perm=[(0, 1), (1, 0)])
    first = lax.axis_index("fsdp") == 0
    low = jnp.where(first, own, other)
    high = jnp.where(first, other, own)
    return jnp.concatenate([low, high], axis=axis)


def pair_scatter(term, axis):
    half = term.shape[axis] // 2
    idx = lax.axis_index("fsdp")
    keep = lax.dynamic_slice_in_dim(term, idx * half, half, axis)
    send = lax.dynamic_slice_in_dim(term, (1 - idx) * half, half, axis)
    recv = lax.ppermute(send, "fsdp", perm=[(0, 1), (1, 0)])
    return keep.astype(jnp.float32) + recv.astype(jnp.float32)


def ring_allreduce(flat, axis, size):
    me = lax.axis_index(axis)
    halves = flat.reshape(2, size, -1)
    fwd = [(i, (i + 1) % size) for i in range(size)]
    bwd = [(i, (i - 1) % size) for i in range(size)]
    parts = []
    for direction, perm in ((1, fwd), (-1, bwd)):
        chunks = halves[0 if direction == 1 else 1]
        acc = lax.dynamic_index_in_dim(chunks, me % size, 0, keepdims=False)
        for step in range(size - 1):
            recv = lax.ppermute(acc.astype(jnp.bfloat16), axis, perm=perm)
            src = (me - direction * (step + 1)) % size
            acc = recv.astype(jnp.float32) + lax.dynamic_index_in_dim(
                chunks, src, 0, keepdims=False
            )
        owned = (me - direction * (size - 1)) % size
        pieces = [acc.astype(jnp.bfloat16)]
        for step in range(size - 1):
            pieces.append(lax.ppermute(pieces[-1], axis, perm=perm))
        values = [lax.reduce_precision(acc, exponent_bits=8, mantissa_bits=7)]
        values += [p.astype(jnp.float32) for p in pieces[1:]]
        if direction == 1:
            values = [values[0]] + values[1:][::-1]
        doubled = jnp.stack(values + values)
        parts.append(lax.dynamic_slice_in_dim(doubled, (size - owned) % size, size, 0))
    return jnp.stack(parts).reshape(flat.shape)


def butterfly_sum(values, axis, size):
    bit = 1
    while bit < size:
        perm = [(i, i ^ bit) for i in range(size)]
        values = values + lax.ppermute(values, axis, perm=perm)
        bit *= 2
    return values


def on_device(
    sizes,
    tokens, cotangent, frame_mask, ln_gain, ln_bias, weight_in, weight_out, blocks_in, blocks_out
):
    frames = tokens.shape[0]
    stacked = jnp.concatenate(
        [tokens, ln_gain[None], ln_bias[None], jnp.zeros((6, tokens.shape[1]), tokens.dtype)]
    )
    gathered = lax.all_to_all(
        jnp.tile(stacked, (1, sizes["tp"])), "tp", split_axis=1, concat_axis=1, tiled=True
    )
    whole_rows = gathered[:frames]
    gain_full, bias_full = gathered[frames], gathered[frames + 1]
    masked_in = apply_blocks(weight_in, blocks_in, jnp.bfloat16)
    masked_out = apply_blocks(weight_out, blocks_out, jnp.bfloat16)
    full_in = pair_gather(masked_in, 0)
    full_out = pair_gather(masked_out, 1)
    width = whole_rows.shape[1]
    own_width = tokens.shape[1]
    col_start = lax.axis_index("tp") * own_width
    gelu_exact = partial(jax.nn.gelu, approximate=False)
    values = whole_rows.astype(jnp.float32)
    centre = jnp.mean(values, axis=1, keepdims=True)
    centred = values - centre
    inv_std = lax.rsqrt(jnp.mean(centred * centred, axis=1, keepdims=True) + 1e-05)
    normed = centred * inv_std
    gain_f = gain_full.astype(jnp.float32)
    scaled = (normed * gain_f + bias_full.astype(jnp.float32)).astype(jnp.bfloat16)
    hidden = jnp.dot(scaled, full_in, preferred_element_type=jnp.float32)
    active = gelu_exact(hidden).astype(jnp.bfloat16)
    partial_out = lax.dot_general(
        full_out, active, (((0,), (1,)), ((), ())), preferred_element_type=jnp.float32
    ).astype(jnp.bfloat16)
    whole_grad = lax.all_gather(cotangent, "tp", axis=1, tiled=True)
    unused, whole_grad = lax.optimization_barrier((partial_out, whole_grad))
    branch = lax.psum_scatter(
        partial_out, "tp", scatter_dimension=0, tiled=True
    ).astype(jnp.float32).T
    flags = frame_mask[:, None].astype(jnp.bfloat16)
    chosen = whole_grad * flags
    chosen_own = cotangent * flags
    back_active = contract_cols(chosen, full_out)
    unused, gelu_back = jax.vjp(gelu_exact, hidden)
    back_hidden = gelu_back(back_active)[0].astype(jnp.bfloat16)
    partial_normed = contract_cols(back_hidden, full_in).astype(jnp.bfloat16)
    back_normed = lax.psum_scatter(
        partial_normed, "tp", scatter_dimension=1, tiled=True
    ).astype(jnp.float32)
    piece = partial_normed.astype(jnp.float32)
    piece_scaled = piece * gain_f
    row_sums = jnp.stack([jnp.sum(piece_scaled, axis=1), jnp.sum(piece_scaled * normed, axis=1)])
    col_sums = jnp.stack([jnp.sum(piece * normed, axis=0), jnp.sum(piece, axis=0)])
    both_sums = butterfly_sum(jnp.concatenate([row_sums, col_sums], axis=1), "tp", sizes["tp"])
    row_sums, col_sums = both_sums[:, :frames], both_sums[:, frames:]
    sum_plain, sum_cross = row_sums[0], row_sums[1]
    for name in ("fsdp", "rep"):
        col_sums = butterfly_sum(col_sums, name, sizes[name])
    whole_gain, whole_bias = col_sums[0], col_sums[1]
    grad_gain = lax.dynamic_slice_in_dim(whole_gain, col_start, own_width, 0)
    grad_bias = lax.dynamic_slice_in_dim(whole_bias, col_start, own_width, 0)
    term_in = contract_rows(scaled, back_hidden).astype(jnp.bfloat16)
    term_out = contract_rows(active, chosen).astype(jnp.bfloat16)
    shard_in = pair_scatter(term_in, 0)
    shard_out = pair_scatter(term_out, 1)
    both = jnp.concatenate([shard_in.reshape(-1), shard_out.reshape(-1)])
    both, branch = lax.optimization_barrier((both, branch))
    block_out = (tokens.astype(jnp.float32) + branch).astype(jnp.bfloat16)
    total = ring_allreduce(both, "rep", sizes["rep"])
    shard_in = total[: shard_in.size].reshape(shard_in.shape)
    shard_out = total[shard_in.size :].reshape(shard_out.shape)
    grad_in = apply_blocks(shard_in, blocks_in, jnp.float32)
    grad_out = apply_blocks(shard_out, blocks_out, jnp.float32)
    grad_in, grad_out, back_normed = lax.optimization_barrier((grad_in, grad_out, back_normed))
    normed_own = lax.dynamic_slice_in_dim(normed, col_start, own_width, 1)
    gain_own = ln_gain.astype(jnp.float32)
    back_scaled = back_normed * gain_own
    mean_plain = (sum_plain / width)[:, None]
    mean_cross = (sum_cross / width)[:, None]
    back_rows = inv_std * (back_scaled - mean_plain - normed_own * mean_cross)
    input_grad = (chosen_own.astype(jnp.float32) + back_rows).astype(jnp.bfloat16)
    return (block_out, input_grad, grad_in, grad_out, grad_gain, grad_bias)


def solution(mesh):
    placed = (
        P(("rep", "fsdp"), "tp"),
        P(("rep", "fsdp"), "tp"),
        P(("rep", "fsdp")),
        P("tp"),
        P("tp"),
        P("fsdp", "tp"),
        P("tp", "fsdp"),
        P("fsdp", "tp"),
        P("tp", "fsdp"),
    )
    return jax.shard_map(
        partial(on_device, dict(mesh.shape)),
        mesh=mesh,
        in_specs=placed,
        out_specs=(
            P(("rep", "fsdp"), "tp"),
            P(("rep", "fsdp"), "tp"),
            P("fsdp", "tp"),
            P("tp", "fsdp"),
            P("tp"),
            P("tp"),
        ),
        check_vma=False,
    )
```

```python
from functools import partial

import jax
import jax.numpy as jnp
from jax import lax
from jax.sharding import PartitionSpec as P

BLK = 128


def apply_blocks(weight, blocks, kind):
    row_blocks, col_blocks = blocks.shape
    shaped = weight.reshape(row_blocks, BLK, col_blocks, BLK)
    keeper = blocks.astype(kind)[:, None, :, None]
    return (shaped * keeper).reshape(weight.shape)


def contract_rows(left, right):
    return lax.dot_general(
        left, right, (((0,), (0,)), ((), ())), preferred_element_type=jnp.float32
    )


def contract_cols(left, right):
    return lax.dot_general(
        left, right, (((1,), (1,)), ((), ())), preferred_element_type=jnp.float32
    )


def pair_gather(own, axis):
    other = lax.ppermute(own, "fsdp", perm=[(0, 1), (1, 0)])
    first = lax.axis_index("fsdp") == 0
    low = jnp.where(first, own, other)
    high = jnp.where(first, other, own)
    return jnp.concatenate([low, high], axis=axis)


def pair_scatter(term, axis):
    half = term.shape[axis] // 2
    idx = lax.axis_index("fsdp")
    keep = lax.dynamic_slice_in_dim(term, idx * half, half, axis)
    send = lax.dynamic_slice_in_dim(term, (1 - idx) * half, half, axis)
    recv = lax.ppermute(send, "fsdp", perm=[(0, 1), (1, 0)])
    return keep.astype(jnp.float32) + recv.astype(jnp.float32)


def chunk_allreduce(flat, axis, size):
    chunks = flat.astype(jnp.bfloat16).reshape(size, -1)
    mine = lax.all_to_all(chunks, axis, split_axis=0, concat_axis=0, tiled=True)
    reduced = jnp.sum(mine.astype(jnp.float32), axis=0).astype(jnp.bfloat16)
    copies = jnp.broadcast_to(reduced[None], chunks.shape)
    whole = lax.all_to_all(copies, axis, split_axis=0, concat_axis=0, tiled=True)
    return whole.astype(jnp.float32).reshape(flat.shape)


def butterfly_sum(values, axis, size):
    bit = 1
    while bit < size:
        perm = [(i, i ^ bit) for i in range(size)]
        values = values + lax.ppermute(values, axis, perm=perm)
        bit *= 2
    return values


def on_device(
    sizes,
    tokens, cotangent, frame_mask, ln_gain, ln_bias, weight_in, weight_out, blocks_in, blocks_out
):
    frames = tokens.shape[0]
    stacked = jnp.concatenate(
        [tokens, ln_gain[None], ln_bias[None], jnp.zeros((6, tokens.shape[1]), tokens.dtype)]
    )
    gathered = lax.all_to_all(
        jnp.tile(stacked, (1, sizes["tp"])), "tp", split_axis=1, concat_axis=1, tiled=True
    )
    whole_rows = gathered[:frames]
    gain_full, bias_full = gathered[frames], gathered[frames + 1]
    masked_in = apply_blocks(weight_in, blocks_in, jnp.bfloat16)
    masked_out = apply_blocks(weight_out, blocks_out, jnp.bfloat16)
    full_in = pair_gather(masked_in, 0)
    full_out = pair_gather(masked_out, 1)
    width = whole_rows.shape[1]
    own_width = tokens.shape[1]
    col_start = lax.axis_index("tp") * own_width
    gelu_exact = partial(jax.nn.gelu, approximate=False)
    values = whole_rows.astype(jnp.float32)
    centre = jnp.mean(values, axis=1, keepdims=True)
    centred = values - centre
    inv_std = lax.rsqrt(jnp.mean(centred * centred, axis=1, keepdims=True) + 1e-05)
    normed = centred * inv_std
    gain_f = gain_full.astype(jnp.float32)
    scaled = (normed * gain_f + bias_full.astype(jnp.float32)).astype(jnp.bfloat16)
    hidden = jnp.dot(scaled, full_in, preferred_element_type=jnp.float32)
    active = gelu_exact(hidden).astype(jnp.bfloat16)
    partial_out = lax.dot_general(
        full_out, active, (((0,), (1,)), ((), ())), preferred_element_type=jnp.float32
    ).astype(jnp.bfloat16)
    whole_grad = lax.all_gather(cotangent, "tp", axis=1, tiled=True)
    unused, whole_grad = lax.optimization_barrier((partial_out, whole_grad))
    branch = lax.psum_scatter(
        partial_out, "tp", scatter_dimension=0, tiled=True
    ).astype(jnp.float32).T
    flags = frame_mask[:, None].astype(jnp.bfloat16)
    chosen = whole_grad * flags
    chosen_own = cotangent * flags
    back_active = contract_cols(chosen, full_out)
    unused, gelu_back = jax.vjp(gelu_exact, hidden)
    back_hidden = gelu_back(back_active)[0].astype(jnp.bfloat16)
    partial_normed = contract_cols(back_hidden, full_in).astype(jnp.bfloat16)
    back_normed = lax.psum_scatter(
        partial_normed, "tp", scatter_dimension=1, tiled=True
    ).astype(jnp.float32)
    piece = partial_normed.astype(jnp.float32)
    piece_scaled = piece * gain_f
    row_sums = jnp.stack([jnp.sum(piece_scaled, axis=1), jnp.sum(piece_scaled * normed, axis=1)])
    col_sums = jnp.stack([jnp.sum(piece * normed, axis=0), jnp.sum(piece, axis=0)])
    both_sums = butterfly_sum(jnp.concatenate([row_sums, col_sums], axis=1), "tp", sizes["tp"])
    row_sums, col_sums = both_sums[:, :frames], both_sums[:, frames:]
    sum_plain, sum_cross = row_sums[0], row_sums[1]
    for name in ("fsdp", "rep"):
        col_sums = butterfly_sum(col_sums, name, sizes[name])
    whole_gain, whole_bias = col_sums[0], col_sums[1]
    grad_gain = lax.dynamic_slice_in_dim(whole_gain, col_start, own_width, 0)
    grad_bias = lax.dynamic_slice_in_dim(whole_bias, col_start, own_width, 0)
    term_in = contract_rows(scaled, back_hidden).astype(jnp.bfloat16)
    term_out = contract_rows(active, chosen).astype(jnp.bfloat16)
    shard_in = pair_scatter(term_in, 0)
    shard_out = pair_scatter(term_out, 1)
    both = jnp.concatenate([shard_in.reshape(-1), shard_out.reshape(-1)])
    both, branch = lax.optimization_barrier((both, branch))
    block_out = (tokens.astype(jnp.float32) + branch).astype(jnp.bfloat16)
    total = chunk_allreduce(both, "rep", sizes["rep"])
    shard_in = total[: shard_in.size].reshape(shard_in.shape)
    shard_out = total[shard_in.size :].reshape(shard_out.shape)
    grad_in = apply_blocks(shard_in, blocks_in, jnp.float32)
    grad_out = apply_blocks(shard_out, blocks_out, jnp.float32)
    grad_in, grad_out, back_normed = lax.optimization_barrier((grad_in, grad_out, back_normed))
    normed_own = lax.dynamic_slice_in_dim(normed, col_start, own_width, 1)
    gain_own = ln_gain.astype(jnp.float32)
    back_scaled = back_normed * gain_own
    mean_plain = (sum_plain / width)[:, None]
    mean_cross = (sum_cross / width)[:, None]
    back_rows = inv_std * (back_scaled - mean_plain - normed_own * mean_cross)
    input_grad = (chosen_own.astype(jnp.float32) + back_rows).astype(jnp.bfloat16)
    return (block_out, input_grad, grad_in, grad_out, grad_gain, grad_bias)


def solution(mesh):
    placed = (
        P(("rep", "fsdp"), "tp"),
        P(("rep", "fsdp"), "tp"),
        P(("rep", "fsdp")),
        P("tp"),
        P("tp"),
        P("fsdp", "tp"),
        P("tp", "fsdp"),
        P("fsdp", "tp"),
        P("tp", "fsdp"),
    )
    return jax.shard_map(
        partial(on_device, dict(mesh.shape)),
        mesh=mesh,
        in_specs=placed,
        out_specs=(
            P(("rep", "fsdp"), "tp"),
            P(("rep", "fsdp"), "tp"),
            P("fsdp", "tp"),
            P("tp", "fsdp"),
            P("tp"),
            P("tp"),
        ),
        check_vma=False,
    )
```

```python
from functools import partial

import jax
import jax.numpy as jnp
from jax import lax
from jax.sharding import PartitionSpec as P

BLK = 128


def apply_blocks(weight, blocks, kind):
    row_blocks, col_blocks = blocks.shape
    shaped = weight.reshape(row_blocks, BLK, col_blocks, BLK)
    keeper = blocks.astype(kind)[:, None, :, None]
    return (shaped * keeper).reshape(weight.shape)


def contract_rows(left, right):
    return lax.dot_general(
        left, right, (((0,), (0,)), ((), ())), preferred_element_type=jnp.float32
    )


def contract_cols(left, right):
    return lax.dot_general(
        left, right, (((1,), (1,)), ((), ())), preferred_element_type=jnp.float32
    )


def pair_gather(own, axis):
    other = lax.ppermute(own, "fsdp", perm=[(0, 1), (1, 0)])
    first = lax.axis_index("fsdp") == 0
    low = jnp.where(first, own, other)
    high = jnp.where(first, other, own)
    return jnp.concatenate([low, high], axis=axis)


def pair_scatter(term, axis):
    half = term.shape[axis] // 2
    idx = lax.axis_index("fsdp")
    keep = lax.dynamic_slice_in_dim(term, idx * half, half, axis)
    send = lax.dynamic_slice_in_dim(term, (1 - idx) * half, half, axis)
    recv = lax.ppermute(send, "fsdp", perm=[(0, 1), (1, 0)])
    return keep.astype(jnp.float32) + recv.astype(jnp.float32)


def rows_allreduce(term, axis, size):
    rows = term.shape[0] // size
    mine = lax.all_to_all(term.astype(jnp.bfloat16), axis, split_axis=0, concat_axis=0, tiled=True)
    reduced = jnp.sum(mine.reshape(size, rows, -1).astype(jnp.float32), axis=0)
    reduced = reduced.astype(jnp.bfloat16)
    copies = jnp.broadcast_to(reduced[None], (size,) + reduced.shape).reshape(term.shape)
    whole = lax.all_to_all(copies, axis, split_axis=0, concat_axis=0, tiled=True)
    return whole.astype(jnp.float32)


def butterfly_sum(values, axis, size):
    bit = 1
    while bit < size:
        perm = [(i, i ^ bit) for i in range(size)]
        values = values + lax.ppermute(values, axis, perm=perm)
        bit *= 2
    return values


def on_device(
    sizes,
    tokens, cotangent, frame_mask, ln_gain, ln_bias, weight_in, weight_out, blocks_in, blocks_out
):
    frames = tokens.shape[0]
    stacked = jnp.concatenate(
        [tokens, ln_gain[None], ln_bias[None], jnp.zeros((6, tokens.shape[1]), tokens.dtype)]
    )
    gathered = lax.all_to_all(
        jnp.tile(stacked, (1, sizes["tp"])), "tp", split_axis=1, concat_axis=1, tiled=True
    )
    whole_rows = gathered[:frames]
    gain_full, bias_full = gathered[frames], gathered[frames + 1]
    masked_in = apply_blocks(weight_in, blocks_in, jnp.bfloat16)
    masked_out = apply_blocks(weight_out, blocks_out, jnp.bfloat16)
    full_in = pair_gather(masked_in, 0)
    full_out = pair_gather(masked_out, 1)
    width = whole_rows.shape[1]
    own_width = tokens.shape[1]
    col_start = lax.axis_index("tp") * own_width
    gelu_exact = partial(jax.nn.gelu, approximate=False)
    values = whole_rows.astype(jnp.float32)
    centre = jnp.mean(values, axis=1, keepdims=True)
    centred = values - centre
    inv_std = lax.rsqrt(jnp.mean(centred * centred, axis=1, keepdims=True) + 1e-05)
    normed = centred * inv_std
    gain_f = gain_full.astype(jnp.float32)
    scaled = (normed * gain_f + bias_full.astype(jnp.float32)).astype(jnp.bfloat16)
    hidden = jnp.dot(scaled, full_in, preferred_element_type=jnp.float32)
    active = gelu_exact(hidden).astype(jnp.bfloat16)
    partial_out = lax.dot_general(
        full_out, active, (((0,), (1,)), ((), ())), preferred_element_type=jnp.float32
    ).astype(jnp.bfloat16)
    whole_grad = lax.all_gather(cotangent, "tp", axis=1, tiled=True)
    unused, whole_grad = lax.optimization_barrier((partial_out, whole_grad))
    branch = lax.psum_scatter(
        partial_out, "tp", scatter_dimension=0, tiled=True
    ).astype(jnp.float32).T
    flags = frame_mask[:, None].astype(jnp.bfloat16)
    chosen = whole_grad * flags
    chosen_own = cotangent * flags
    back_active = contract_cols(chosen, full_out)
    unused, gelu_back = jax.vjp(gelu_exact, hidden)
    back_hidden = gelu_back(back_active)[0].astype(jnp.bfloat16)
    partial_normed = contract_cols(back_hidden, full_in).astype(jnp.bfloat16)
    back_normed = lax.psum_scatter(
        partial_normed, "tp", scatter_dimension=1, tiled=True
    ).astype(jnp.float32)
    piece = partial_normed.astype(jnp.float32)
    piece_scaled = piece * gain_f
    row_sums = jnp.stack([jnp.sum(piece_scaled, axis=1), jnp.sum(piece_scaled * normed, axis=1)])
    col_sums = jnp.stack([jnp.sum(piece * normed, axis=0), jnp.sum(piece, axis=0)])
    both_sums = butterfly_sum(jnp.concatenate([row_sums, col_sums], axis=1), "tp", sizes["tp"])
    row_sums, col_sums = both_sums[:, :frames], both_sums[:, frames:]
    sum_plain, sum_cross = row_sums[0], row_sums[1]
    for name in ("fsdp", "rep"):
        col_sums = butterfly_sum(col_sums, name, sizes[name])
    whole_gain, whole_bias = col_sums[0], col_sums[1]
    grad_gain = lax.dynamic_slice_in_dim(whole_gain, col_start, own_width, 0)
    grad_bias = lax.dynamic_slice_in_dim(whole_bias, col_start, own_width, 0)
    term_in = contract_rows(scaled, back_hidden).astype(jnp.bfloat16)
    term_out = contract_rows(active, chosen).astype(jnp.bfloat16)
    shard_in = pair_scatter(term_in, 0)
    shard_out = pair_scatter(term_out, 1)
    shard_in, shard_out, branch = lax.optimization_barrier((shard_in, shard_out, branch))
    block_out = (tokens.astype(jnp.float32) + branch).astype(jnp.bfloat16)
    shard_in = rows_allreduce(shard_in, "rep", sizes["rep"])
    shard_out = rows_allreduce(shard_out, "rep", sizes["rep"])
    grad_in = apply_blocks(shard_in, blocks_in, jnp.float32)
    grad_out = apply_blocks(shard_out, blocks_out, jnp.float32)
    grad_in, grad_out, back_normed = lax.optimization_barrier((grad_in, grad_out, back_normed))
    normed_own = lax.dynamic_slice_in_dim(normed, col_start, own_width, 1)
    gain_own = ln_gain.astype(jnp.float32)
    back_scaled = back_normed * gain_own
    mean_plain = (sum_plain / width)[:, None]
    mean_cross = (sum_cross / width)[:, None]
    back_rows = inv_std * (back_scaled - mean_plain - normed_own * mean_cross)
    input_grad = (chosen_own.astype(jnp.float32) + back_rows).astype(jnp.bfloat16)
    return (block_out, input_grad, grad_in, grad_out, grad_gain, grad_bias)


def solution(mesh):
    placed = (
        P(("rep", "fsdp"), "tp"),
        P(("rep", "fsdp"), "tp"),
        P(("rep", "fsdp")),
        P("tp"),
        P("tp"),
        P("fsdp", "tp"),
        P("tp", "fsdp"),
        P("fsdp", "tp"),
        P("tp", "fsdp"),
    )
    return jax.shard_map(
        partial(on_device, dict(mesh.shape)),
        mesh=mesh,
        in_specs=placed,
        out_specs=(
            P(("rep", "fsdp"), "tp"),
            P(("rep", "fsdp"), "tp"),
            P("fsdp", "tp"),
            P("tp", "fsdp"),
            P("tp"),
            P("tp"),
        ),
        check_vma=False,
    )
```

```python
from functools import partial

import jax
import jax.numpy as jnp
from jax import lax
from jax.sharding import PartitionSpec as P

BLK = 128


def apply_blocks(weight, blocks, kind):
    row_blocks, col_blocks = blocks.shape
    shaped = weight.reshape(row_blocks, BLK, col_blocks, BLK)
    keeper = blocks.astype(kind)[:, None, :, None]
    return (shaped * keeper).reshape(weight.shape)


def contract_rows(left, right):
    return lax.dot_general(
        left, right, (((0,), (0,)), ((), ())), preferred_element_type=jnp.float32
    )


def contract_cols(left, right):
    return lax.dot_general(
        left, right, (((1,), (1,)), ((), ())), preferred_element_type=jnp.float32
    )


def pair_gather(own, axis):
    other = lax.ppermute(own, "fsdp", perm=[(0, 1), (1, 0)])
    first = lax.axis_index("fsdp") == 0
    low = jnp.where(first, own, other)
    high = jnp.where(first, other, own)
    return jnp.concatenate([low, high], axis=axis)


def pair_scatter(term, axis):
    half = term.shape[axis] // 2
    idx = lax.axis_index("fsdp")
    keep = lax.dynamic_slice_in_dim(term, idx * half, half, axis)
    send = lax.dynamic_slice_in_dim(term, (1 - idx) * half, half, axis)
    recv = lax.ppermute(send, "fsdp", perm=[(0, 1), (1, 0)])
    return keep.astype(jnp.float32) + recv.astype(jnp.float32)


def rows_allreduce(term, axis, size):
    rows = term.shape[0] // size
    mine = lax.all_to_all(term.astype(jnp.bfloat16), axis, split_axis=0, concat_axis=0, tiled=True)
    reduced = jnp.sum(mine.reshape(size, rows, -1).astype(jnp.float32), axis=0)
    reduced = reduced.astype(jnp.bfloat16)
    copies = jnp.broadcast_to(reduced[None], (size,) + reduced.shape).reshape(term.shape)
    whole = lax.all_to_all(copies, axis, split_axis=0, concat_axis=0, tiled=True)
    return whole.astype(jnp.float32)


def butterfly_sum(values, axis, size):
    bit = 1
    while bit < size:
        perm = [(i, i ^ bit) for i in range(size)]
        values = values + lax.ppermute(values, axis, perm=perm)
        bit *= 2
    return values


def on_device(
    sizes,
    tokens, cotangent, frame_mask, ln_gain, ln_bias, weight_in, weight_out, blocks_in, blocks_out
):
    frames = tokens.shape[0]
    own_width = tokens.shape[1]
    stacked = jnp.concatenate(
        [tokens, ln_gain[None], ln_bias[None], jnp.zeros((6, tokens.shape[1]), tokens.dtype)]
    )
    gathered = lax.all_to_all(
        jnp.tile(stacked, (1, sizes["tp"])), "tp", split_axis=1, concat_axis=1, tiled=True
    )
    whole_rows = gathered[:frames]
    gain_full, bias_full = gathered[frames], gathered[frames + 1]
    masked_in = apply_blocks(weight_in, blocks_in, jnp.bfloat16)
    masked_out = apply_blocks(weight_out, blocks_out, jnp.bfloat16)
    full_in = pair_gather(masked_in, 0)
    full_out = pair_gather(masked_out, 1)
    width = whole_rows.shape[1]
    col_start = lax.axis_index("tp") * own_width
    gelu_exact = partial(jax.nn.gelu, approximate=False)
    values = whole_rows.astype(jnp.float32)
    centre = jnp.mean(values, axis=1, keepdims=True)
    centred = values - centre
    inv_std = lax.rsqrt(jnp.mean(centred * centred, axis=1, keepdims=True) + 1e-05)
    normed = centred * inv_std
    gain_f = gain_full.astype(jnp.float32)
    scaled = (normed * gain_f + bias_full.astype(jnp.float32)).astype(jnp.bfloat16)
    hidden = jnp.dot(scaled, full_in, preferred_element_type=jnp.float32)
    active = gelu_exact(hidden).astype(jnp.bfloat16)
    partial_out = lax.dot_general(
        full_out, active, (((0,), (1,)), ((), ())), preferred_element_type=jnp.float32
    ).astype(jnp.bfloat16)
    whole_grad = lax.all_gather(cotangent, "tp", axis=1, tiled=True)
    unused, whole_grad = lax.optimization_barrier((partial_out, whole_grad))
    half = frames // 2
    first_half = lax.psum_scatter(
        partial_out[:, :half], "tp", scatter_dimension=0, tiled=True
    ).astype(jnp.float32)
    received = lax.all_to_all(partial_out[:, half:], "tp", split_axis=0, concat_axis=0, tiled=True)
    second_half = jnp.sum(
        received.reshape(sizes["tp"], own_width, -1).astype(jnp.float32), axis=0
    )
    branch = jnp.concatenate([first_half, second_half], axis=1).T
    flags = frame_mask[:, None].astype(jnp.bfloat16)
    chosen = whole_grad * flags
    chosen_own = cotangent * flags
    back_active = contract_cols(chosen, full_out)
    unused, gelu_back = jax.vjp(gelu_exact, hidden)
    back_hidden = gelu_back(back_active)[0].astype(jnp.bfloat16)
    partial_normed = contract_cols(back_hidden, full_in).astype(jnp.bfloat16)
    back_normed = lax.psum_scatter(
        partial_normed, "tp", scatter_dimension=1, tiled=True
    ).astype(jnp.float32)
    piece = partial_normed.astype(jnp.float32)
    piece_scaled = piece * gain_f
    row_sums = jnp.stack([jnp.sum(piece_scaled, axis=1), jnp.sum(piece_scaled * normed, axis=1)])
    col_sums = jnp.stack([jnp.sum(piece * normed, axis=0), jnp.sum(piece, axis=0)])
    both_sums = butterfly_sum(jnp.concatenate([row_sums, col_sums], axis=1), "tp", sizes["tp"])
    row_sums, col_sums = both_sums[:, :frames], both_sums[:, frames:]
    sum_plain, sum_cross = row_sums[0], row_sums[1]
    for name in ("fsdp", "rep"):
        col_sums = butterfly_sum(col_sums, name, sizes[name])
    whole_gain, whole_bias = col_sums[0], col_sums[1]
    grad_gain = lax.dynamic_slice_in_dim(whole_gain, col_start, own_width, 0)
    grad_bias = lax.dynamic_slice_in_dim(whole_bias, col_start, own_width, 0)
    term_in = contract_rows(scaled, back_hidden).astype(jnp.bfloat16)
    term_out = contract_rows(active, chosen).astype(jnp.bfloat16)
    shard_in = pair_scatter(term_in, 0)
    shard_out = pair_scatter(term_out, 1)
    shard_in, shard_out, branch = lax.optimization_barrier((shard_in, shard_out, branch))
    block_out = (tokens.astype(jnp.float32) + branch).astype(jnp.bfloat16)
    shard_in = rows_allreduce(shard_in, "rep", sizes["rep"])
    shard_out = rows_allreduce(shard_out, "rep", sizes["rep"])
    grad_in = apply_blocks(shard_in, blocks_in, jnp.float32)
    grad_out = apply_blocks(shard_out, blocks_out, jnp.float32)
    grad_in, grad_out, back_normed = lax.optimization_barrier((grad_in, grad_out, back_normed))
    normed_own = lax.dynamic_slice_in_dim(normed, col_start, own_width, 1)
    gain_own = ln_gain.astype(jnp.float32)
    back_scaled = back_normed * gain_own
    mean_plain = (sum_plain / width)[:, None]
    mean_cross = (sum_cross / width)[:, None]
    back_rows = inv_std * (back_scaled - mean_plain - normed_own * mean_cross)
    input_grad = (chosen_own.astype(jnp.float32) + back_rows).astype(jnp.bfloat16)
    return (block_out, input_grad, grad_in, grad_out, grad_gain, grad_bias)


def solution(mesh):
    placed = (
        P(("rep", "fsdp"), "tp"),
        P(("rep", "fsdp"), "tp"),
        P(("rep", "fsdp")),
        P("tp"),
        P("tp"),
        P("fsdp", "tp"),
        P("tp", "fsdp"),
        P("fsdp", "tp"),
        P("tp", "fsdp"),
    )
    return jax.shard_map(
        partial(on_device, dict(mesh.shape)),
        mesh=mesh,
        in_specs=placed,
        out_specs=(
            P(("rep", "fsdp"), "tp"),
            P(("rep", "fsdp"), "tp"),
            P("fsdp", "tp"),
            P("tp", "fsdp"),
            P("tp"),
            P("tp"),
        ),
        check_vma=False,
    )
```

```python
from functools import partial

import jax
import jax.numpy as jnp
from jax import lax
from jax.sharding import PartitionSpec as P

BLK = 128


def apply_blocks(weight, blocks, kind):
    row_blocks, col_blocks = blocks.shape
    shaped = weight.reshape(row_blocks, BLK, col_blocks, BLK)
    keeper = blocks.astype(kind)[:, None, :, None]
    return (shaped * keeper).reshape(weight.shape)


def contract_rows(left, right):
    return lax.dot_general(
        left, right, (((0,), (0,)), ((), ())), preferred_element_type=jnp.float32
    )


def contract_cols(left, right):
    return lax.dot_general(
        left, right, (((1,), (1,)), ((), ())), preferred_element_type=jnp.float32
    )


def pair_gather(own, axis):
    other = lax.ppermute(own, "fsdp", perm=[(0, 1), (1, 0)])
    first = lax.axis_index("fsdp") == 0
    low = jnp.where(first, own, other)
    high = jnp.where(first, other, own)
    return jnp.concatenate([low, high], axis=axis)


def pair_scatter(term, axis):
    half = term.shape[axis] // 2
    idx = lax.axis_index("fsdp")
    keep = lax.dynamic_slice_in_dim(term, idx * half, half, axis)
    send = lax.dynamic_slice_in_dim(term, (1 - idx) * half, half, axis)
    recv = lax.ppermute(send, "fsdp", perm=[(0, 1), (1, 0)])
    return keep.astype(jnp.float32) + recv.astype(jnp.float32)


def rows_allreduce(term, axis, size):
    rows = term.shape[0] // size
    mine = lax.all_to_all(term.astype(jnp.bfloat16), axis, split_axis=0, concat_axis=0, tiled=True)
    reduced = jnp.sum(mine.reshape(size, rows, -1).astype(jnp.float32), axis=0)
    reduced = reduced.astype(jnp.bfloat16)
    copies = jnp.broadcast_to(reduced[None], (size,) + reduced.shape).reshape(term.shape)
    whole = lax.all_to_all(copies, axis, split_axis=0, concat_axis=0, tiled=True)
    return whole.astype(jnp.float32)


def butterfly_sum(values, axis, size):
    bit = 1
    while bit < size:
        perm = [(i, i ^ bit) for i in range(size)]
        values = values + lax.ppermute(values, axis, perm=perm)
        bit *= 2
    return values


def on_device(
    sizes,
    tokens, cotangent, frame_mask, ln_gain, ln_bias, weight_in, weight_out, blocks_in, blocks_out
):
    frames = tokens.shape[0]
    own_width = tokens.shape[1]
    stacked = jnp.concatenate(
        [tokens, ln_gain[None], ln_bias[None], jnp.zeros((6, tokens.shape[1]), tokens.dtype)]
    )
    gathered = lax.all_to_all(
        jnp.tile(stacked, (1, sizes["tp"])), "tp", split_axis=1, concat_axis=1, tiled=True
    )
    whole_rows = gathered[:frames]
    gain_full, bias_full = gathered[frames], gathered[frames + 1]
    masked_in = apply_blocks(weight_in, blocks_in, jnp.bfloat16)
    masked_out = apply_blocks(weight_out, blocks_out, jnp.bfloat16)
    full_in = pair_gather(masked_in, 0)
    full_out = pair_gather(masked_out, 1)
    width = whole_rows.shape[1]
    col_start = lax.axis_index("tp") * own_width
    gelu_exact = partial(jax.nn.gelu, approximate=False)
    values = whole_rows.astype(jnp.float32)
    centre = jnp.mean(values, axis=1, keepdims=True)
    centred = values - centre
    inv_std = lax.rsqrt(jnp.mean(centred * centred, axis=1, keepdims=True) + 1e-05)
    normed = centred * inv_std
    gain_f = gain_full.astype(jnp.float32)
    scaled = (normed * gain_f + bias_full.astype(jnp.float32)).astype(jnp.bfloat16)
    hidden = jnp.dot(scaled, full_in, preferred_element_type=jnp.float32)
    active = gelu_exact(hidden).astype(jnp.bfloat16)
    partial_out = lax.dot_general(
        full_out, active, (((0,), (1,)), ((), ())), preferred_element_type=jnp.float32
    ).astype(jnp.bfloat16)
    whole_grad = lax.all_to_all(
        jnp.tile(cotangent, (1, sizes["tp"])), "tp", split_axis=1, concat_axis=1, tiled=True
    )
    unused, whole_grad = lax.optimization_barrier((partial_out, whole_grad))
    received = lax.all_to_all(partial_out, "tp", split_axis=0, concat_axis=0, tiled=True)
    branch = jnp.sum(
        received.reshape(sizes["tp"], own_width, -1).astype(jnp.float32), axis=0
    ).T
    flags = frame_mask[:, None].astype(jnp.bfloat16)
    chosen = whole_grad * flags
    chosen_own = cotangent * flags
    back_active = contract_cols(chosen, full_out)
    unused, gelu_back = jax.vjp(gelu_exact, hidden)
    back_hidden = gelu_back(back_active)[0].astype(jnp.bfloat16)
    partial_normed = contract_cols(back_hidden, full_in).astype(jnp.bfloat16)
    received = lax.all_to_all(partial_normed, "tp", split_axis=1, concat_axis=0, tiled=True)
    back_normed = jnp.sum(
        received.reshape(sizes["tp"], frames, -1).astype(jnp.float32), axis=0
    )
    piece = partial_normed.astype(jnp.float32)
    piece_scaled = piece * gain_f
    row_sums = jnp.stack([jnp.sum(piece_scaled, axis=1), jnp.sum(piece_scaled * normed, axis=1)])
    col_sums = jnp.stack([jnp.sum(piece * normed, axis=0), jnp.sum(piece, axis=0)])
    both_sums = butterfly_sum(jnp.concatenate([row_sums, col_sums], axis=1), "tp", sizes["tp"])
    row_sums, col_sums = both_sums[:, :frames], both_sums[:, frames:]
    sum_plain, sum_cross = row_sums[0], row_sums[1]
    for name in ("fsdp", "rep"):
        col_sums = butterfly_sum(col_sums, name, sizes[name])
    whole_gain, whole_bias = col_sums[0], col_sums[1]
    grad_gain = lax.dynamic_slice_in_dim(whole_gain, col_start, own_width, 0)
    grad_bias = lax.dynamic_slice_in_dim(whole_bias, col_start, own_width, 0)
    term_in = contract_rows(scaled, back_hidden).astype(jnp.bfloat16)
    term_out = contract_rows(active, chosen).astype(jnp.bfloat16)
    shard_in = pair_scatter(term_in, 0)
    shard_out = pair_scatter(term_out, 1)
    shard_in, shard_out, branch = lax.optimization_barrier((shard_in, shard_out, branch))
    block_out = (tokens.astype(jnp.float32) + branch).astype(jnp.bfloat16)
    shard_in = rows_allreduce(shard_in, "rep", sizes["rep"])
    shard_out = rows_allreduce(shard_out, "rep", sizes["rep"])
    grad_in = apply_blocks(shard_in, blocks_in, jnp.float32)
    grad_out = apply_blocks(shard_out, blocks_out, jnp.float32)
    grad_in, grad_out, back_normed = lax.optimization_barrier((grad_in, grad_out, back_normed))
    normed_own = lax.dynamic_slice_in_dim(normed, col_start, own_width, 1)
    gain_own = ln_gain.astype(jnp.float32)
    back_scaled = back_normed * gain_own
    mean_plain = (sum_plain / width)[:, None]
    mean_cross = (sum_cross / width)[:, None]
    back_rows = inv_std * (back_scaled - mean_plain - normed_own * mean_cross)
    input_grad = (chosen_own.astype(jnp.float32) + back_rows).astype(jnp.bfloat16)
    return (block_out, input_grad, grad_in, grad_out, grad_gain, grad_bias)


def solution(mesh):
    placed = (
        P(("rep", "fsdp"), "tp"),
        P(("rep", "fsdp"), "tp"),
        P(("rep", "fsdp")),
        P("tp"),
        P("tp"),
        P("fsdp", "tp"),
        P("tp", "fsdp"),
        P("fsdp", "tp"),
        P("tp", "fsdp"),
    )
    return jax.shard_map(
        partial(on_device, dict(mesh.shape)),
        mesh=mesh,
        in_specs=placed,
        out_specs=(
            P(("rep", "fsdp"), "tp"),
            P(("rep", "fsdp"), "tp"),
            P("fsdp", "tp"),
            P("tp", "fsdp"),
            P("tp"),
            P("tp"),
        ),
        check_vma=False,
    )
```

```python
from functools import partial

import jax
import jax.numpy as jnp
from jax import lax
from jax.sharding import PartitionSpec as P

BLK = 128


def apply_blocks(weight, blocks, kind):
    row_blocks, col_blocks = blocks.shape
    shaped = weight.reshape(row_blocks, BLK, col_blocks, BLK)
    keeper = blocks.astype(kind)[:, None, :, None]
    return (shaped * keeper).reshape(weight.shape)


def contract_rows(left, right):
    return lax.dot_general(
        left, right, (((0,), (0,)), ((), ())), preferred_element_type=jnp.float32
    )


def contract_cols(left, right):
    return lax.dot_general(
        left, right, (((1,), (1,)), ((), ())), preferred_element_type=jnp.float32
    )


def pair_gather(own, axis):
    other = lax.ppermute(own, "fsdp", perm=[(0, 1), (1, 0)])
    first = lax.axis_index("fsdp") == 0
    low = jnp.where(first, own, other)
    high = jnp.where(first, other, own)
    return jnp.concatenate([low, high], axis=axis)


def pair_scatter(term, axis):
    half = term.shape[axis] // 2
    idx = lax.axis_index("fsdp")
    keep = lax.dynamic_slice_in_dim(term, idx * half, half, axis)
    send = lax.dynamic_slice_in_dim(term, (1 - idx) * half, half, axis)
    recv = lax.ppermute(send, "fsdp", perm=[(0, 1), (1, 0)])
    return keep.astype(jnp.float32) + recv.astype(jnp.float32)


def rows_allreduce(term, axis, size):
    rows = term.shape[0] // size
    mine = lax.all_to_all(term.astype(jnp.bfloat16), axis, split_axis=0, concat_axis=0, tiled=True)
    reduced = jnp.sum(mine.reshape(size, rows, -1).astype(jnp.float32), axis=0)
    reduced = reduced.astype(jnp.bfloat16)
    copies = jnp.broadcast_to(reduced[None], (size,) + reduced.shape).reshape(term.shape)
    whole = lax.all_to_all(copies, axis, split_axis=0, concat_axis=0, tiled=True)
    return whole.astype(jnp.float32)


def butterfly_sum(values, axis, size):
    bit = 1
    while bit < size:
        perm = [(i, i ^ bit) for i in range(size)]
        values = values + lax.ppermute(values, axis, perm=perm)
        bit *= 2
    return values


def on_device(
    sizes,
    tokens, cotangent, frame_mask, ln_gain, ln_bias, weight_in, weight_out, blocks_in, blocks_out
):
    frames = tokens.shape[0]
    stacked = jnp.concatenate(
        [tokens, ln_gain[None], ln_bias[None], jnp.zeros((6, tokens.shape[1]), tokens.dtype)]
    )
    gathered = lax.all_gather(stacked, "tp", axis=1, tiled=True)
    whole_rows = gathered[:frames]
    gain_full, bias_full = gathered[frames], gathered[frames + 1]
    cot_copies, whole_rows = lax.optimization_barrier(
        (jnp.tile(cotangent, (1, sizes["tp"])), whole_rows)
    )
    whole_grad = lax.all_to_all(cot_copies, "tp", split_axis=1, concat_axis=1, tiled=True)
    masked_in = apply_blocks(weight_in, blocks_in, jnp.bfloat16)
    masked_out = apply_blocks(weight_out, blocks_out, jnp.bfloat16)
    full_in = pair_gather(masked_in, 0)
    full_out = pair_gather(masked_out, 1)
    width = whole_rows.shape[1]
    own_width = tokens.shape[1]
    col_start = lax.axis_index("tp") * own_width
    gelu_exact = partial(jax.nn.gelu, approximate=False)
    values = whole_rows.astype(jnp.float32)
    centre = jnp.mean(values, axis=1, keepdims=True)
    centred = values - centre
    inv_std = lax.rsqrt(jnp.mean(centred * centred, axis=1, keepdims=True) + 1e-05)
    normed = centred * inv_std
    gain_f = gain_full.astype(jnp.float32)
    scaled = (normed * gain_f + bias_full.astype(jnp.float32)).astype(jnp.bfloat16)
    hidden = jnp.dot(scaled, full_in, preferred_element_type=jnp.float32)
    active = gelu_exact(hidden).astype(jnp.bfloat16)
    partial_out = lax.dot_general(
        full_out, active, (((0,), (1,)), ((), ())), preferred_element_type=jnp.float32
    ).astype(jnp.bfloat16)
    unused, whole_grad = lax.optimization_barrier((partial_out, whole_grad))
    branch = lax.psum_scatter(
        partial_out, "tp", scatter_dimension=0, tiled=True
    ).astype(jnp.float32).T
    flags = frame_mask[:, None].astype(jnp.bfloat16)
    chosen = whole_grad * flags
    chosen_own = cotangent * flags
    back_active = contract_cols(chosen, full_out)
    unused, gelu_back = jax.vjp(gelu_exact, hidden)
    back_hidden = gelu_back(back_active)[0].astype(jnp.bfloat16)
    partial_normed = contract_cols(back_hidden, full_in).astype(jnp.bfloat16)
    back_normed = lax.psum_scatter(
        partial_normed, "tp", scatter_dimension=1, tiled=True
    ).astype(jnp.float32)
    piece = partial_normed.astype(jnp.float32)
    piece_scaled = piece * gain_f
    row_sums = jnp.stack([jnp.sum(piece_scaled, axis=1), jnp.sum(piece_scaled * normed, axis=1)])
    col_sums = jnp.stack([jnp.sum(piece * normed, axis=0), jnp.sum(piece, axis=0)])
    both_sums = butterfly_sum(jnp.concatenate([row_sums, col_sums], axis=1), "tp", sizes["tp"])
    row_sums, col_sums = both_sums[:, :frames], both_sums[:, frames:]
    sum_plain, sum_cross = row_sums[0], row_sums[1]
    for name in ("fsdp", "rep"):
        col_sums = butterfly_sum(col_sums, name, sizes[name])
    whole_gain, whole_bias = col_sums[0], col_sums[1]
    grad_gain = lax.dynamic_slice_in_dim(whole_gain, col_start, own_width, 0)
    grad_bias = lax.dynamic_slice_in_dim(whole_bias, col_start, own_width, 0)
    term_in = contract_rows(scaled, back_hidden).astype(jnp.bfloat16)
    term_out = contract_rows(active, chosen).astype(jnp.bfloat16)
    shard_in = pair_scatter(term_in, 0)
    shard_out = pair_scatter(term_out, 1)
    shard_in, shard_out, branch = lax.optimization_barrier((shard_in, shard_out, branch))
    block_out = (tokens.astype(jnp.float32) + branch).astype(jnp.bfloat16)
    shard_in = rows_allreduce(shard_in, "rep", sizes["rep"])
    shard_out = rows_allreduce(shard_out, "rep", sizes["rep"])
    grad_in = apply_blocks(shard_in, blocks_in, jnp.float32)
    grad_out = apply_blocks(shard_out, blocks_out, jnp.float32)
    grad_in, grad_out, back_normed = lax.optimization_barrier((grad_in, grad_out, back_normed))
    normed_own = lax.dynamic_slice_in_dim(normed, col_start, own_width, 1)
    gain_own = ln_gain.astype(jnp.float32)
    back_scaled = back_normed * gain_own
    mean_plain = (sum_plain / width)[:, None]
    mean_cross = (sum_cross / width)[:, None]
    back_rows = inv_std * (back_scaled - mean_plain - normed_own * mean_cross)
    input_grad = (chosen_own.astype(jnp.float32) + back_rows).astype(jnp.bfloat16)
    return (block_out, input_grad, grad_in, grad_out, grad_gain, grad_bias)


def solution(mesh):
    placed = (
        P(("rep", "fsdp"), "tp"),
        P(("rep", "fsdp"), "tp"),
        P(("rep", "fsdp")),
        P("tp"),
        P("tp"),
        P("fsdp", "tp"),
        P("tp", "fsdp"),
        P("fsdp", "tp"),
        P("tp", "fsdp"),
    )
    return jax.shard_map(
        partial(on_device, dict(mesh.shape)),
        mesh=mesh,
        in_specs=placed,
        out_specs=(
            P(("rep", "fsdp"), "tp"),
            P(("rep", "fsdp"), "tp"),
            P("fsdp", "tp"),
            P("tp", "fsdp"),
            P("tp"),
            P("tp"),
        ),
        check_vma=False,
    )
```

```python
from functools import partial

import jax
import jax.numpy as jnp
from jax import lax
from jax.sharding import PartitionSpec as P

BLK = 128


def apply_blocks(weight, blocks, kind):
    row_blocks, col_blocks = blocks.shape
    shaped = weight.reshape(row_blocks, BLK, col_blocks, BLK)
    keeper = blocks.astype(kind)[:, None, :, None]
    return (shaped * keeper).reshape(weight.shape)


def contract_rows(left, right):
    return lax.dot_general(
        left, right, (((0,), (0,)), ((), ())), preferred_element_type=jnp.float32
    )


def contract_cols(left, right):
    return lax.dot_general(
        left, right, (((1,), (1,)), ((), ())), preferred_element_type=jnp.float32
    )


def pair_gather(own, axis):
    other = lax.ppermute(own, "fsdp", perm=[(0, 1), (1, 0)])
    first = lax.axis_index("fsdp") == 0
    low = jnp.where(first, own, other)
    high = jnp.where(first, other, own)
    return jnp.concatenate([low, high], axis=axis)


def pair_scatter(term, axis):
    half = term.shape[axis] // 2
    idx = lax.axis_index("fsdp")
    keep = lax.dynamic_slice_in_dim(term, idx * half, half, axis)
    send = lax.dynamic_slice_in_dim(term, (1 - idx) * half, half, axis)
    recv = lax.ppermute(send, "fsdp", perm=[(0, 1), (1, 0)])
    return keep.astype(jnp.float32) + recv.astype(jnp.float32)


def rows_allreduce(term, axis, size):
    rows = term.shape[0] // size
    mine = lax.all_to_all(term.astype(jnp.bfloat16), axis, split_axis=0, concat_axis=0, tiled=True)
    reduced = jnp.sum(mine.reshape(size, rows, -1).astype(jnp.float32), axis=0)
    reduced = reduced.astype(jnp.bfloat16)
    copies = jnp.broadcast_to(reduced[None], (size,) + reduced.shape).reshape(term.shape)
    whole = lax.all_to_all(copies, axis, split_axis=0, concat_axis=0, tiled=True)
    return whole.astype(jnp.float32)


def butterfly_sum(values, axis, size):
    bit = 1
    while bit < size:
        perm = [(i, i ^ bit) for i in range(size)]
        values = values + lax.ppermute(values, axis, perm=perm)
        bit *= 2
    return values


def on_device(
    sizes,
    tokens, cotangent, frame_mask, ln_gain, ln_bias, weight_in, weight_out, blocks_in, blocks_out
):
    frames = tokens.shape[0]
    stacked = jnp.concatenate(
        [tokens, ln_gain[None], ln_bias[None], jnp.zeros((6, tokens.shape[1]), tokens.dtype)]
    )
    copies = jnp.broadcast_to(stacked[None], (sizes["tp"],) + stacked.shape)
    gathered = lax.all_to_all(copies, "tp", split_axis=0, concat_axis=0, tiled=True)
    gathered = jnp.transpose(gathered, (1, 0, 2)).reshape(stacked.shape[0], -1)
    whole_rows = gathered[:frames]
    gain_full, bias_full = gathered[frames], gathered[frames + 1]
    masked_in = apply_blocks(weight_in, blocks_in, jnp.bfloat16)
    masked_out = apply_blocks(weight_out, blocks_out, jnp.bfloat16)
    full_in = pair_gather(masked_in, 0)
    full_out = pair_gather(masked_out, 1)
    width = whole_rows.shape[1]
    own_width = tokens.shape[1]
    col_start = lax.axis_index("tp") * own_width
    gelu_exact = partial(jax.nn.gelu, approximate=False)
    values = whole_rows.astype(jnp.float32)
    centre = jnp.mean(values, axis=1, keepdims=True)
    centred = values - centre
    inv_std = lax.rsqrt(jnp.mean(centred * centred, axis=1, keepdims=True) + 1e-05)
    normed = centred * inv_std
    gain_f = gain_full.astype(jnp.float32)
    scaled = (normed * gain_f + bias_full.astype(jnp.float32)).astype(jnp.bfloat16)
    hidden = jnp.dot(scaled, full_in, preferred_element_type=jnp.float32)
    active = gelu_exact(hidden).astype(jnp.bfloat16)
    partial_out = lax.dot_general(
        full_out, active, (((0,), (1,)), ((), ())), preferred_element_type=jnp.float32
    ).astype(jnp.bfloat16)
    whole_grad = lax.all_gather(cotangent, "tp", axis=1, tiled=True)
    unused, whole_grad = lax.optimization_barrier((partial_out, whole_grad))
    branch = lax.psum_scatter(
        partial_out, "tp", scatter_dimension=0, tiled=True
    ).astype(jnp.float32).T
    flags = frame_mask[:, None].astype(jnp.bfloat16)
    chosen = whole_grad * flags
    chosen_own = cotangent * flags
    back_active = contract_cols(chosen, full_out)
    unused, gelu_back = jax.vjp(gelu_exact, hidden)
    back_hidden = gelu_back(back_active)[0].astype(jnp.bfloat16)
    partial_normed = contract_cols(back_hidden, full_in).astype(jnp.bfloat16)
    back_normed = lax.psum_scatter(
        partial_normed, "tp", scatter_dimension=1, tiled=True
    ).astype(jnp.float32)
    piece = partial_normed.astype(jnp.float32)
    piece_scaled = piece * gain_f
    row_sums = jnp.stack([jnp.sum(piece_scaled, axis=1), jnp.sum(piece_scaled * normed, axis=1)])
    col_sums = jnp.stack([jnp.sum(piece * normed, axis=0), jnp.sum(piece, axis=0)])
    both_sums = butterfly_sum(jnp.concatenate([row_sums, col_sums], axis=1), "tp", sizes["tp"])
    row_sums, col_sums = both_sums[:, :frames], both_sums[:, frames:]
    sum_plain, sum_cross = row_sums[0], row_sums[1]
    for name in ("fsdp", "rep"):
        col_sums = butterfly_sum(col_sums, name, sizes[name])
    whole_gain, whole_bias = col_sums[0], col_sums[1]
    grad_gain = lax.dynamic_slice_in_dim(whole_gain, col_start, own_width, 0)
    grad_bias = lax.dynamic_slice_in_dim(whole_bias, col_start, own_width, 0)
    term_in = contract_rows(scaled, back_hidden).astype(jnp.bfloat16)
    term_out = contract_rows(active, chosen).astype(jnp.bfloat16)
    shard_in = pair_scatter(term_in, 0)
    shard_out = pair_scatter(term_out, 1)
    shard_in, shard_out, branch = lax.optimization_barrier((shard_in, shard_out, branch))
    block_out = (tokens.astype(jnp.float32) + branch).astype(jnp.bfloat16)
    shard_in = rows_allreduce(shard_in, "rep", sizes["rep"])
    shard_out = rows_allreduce(shard_out, "rep", sizes["rep"])
    grad_in = apply_blocks(shard_in, blocks_in, jnp.float32)
    grad_out = apply_blocks(shard_out, blocks_out, jnp.float32)
    grad_in, grad_out, back_normed = lax.optimization_barrier((grad_in, grad_out, back_normed))
    normed_own = lax.dynamic_slice_in_dim(normed, col_start, own_width, 1)
    gain_own = ln_gain.astype(jnp.float32)
    back_scaled = back_normed * gain_own
    mean_plain = (sum_plain / width)[:, None]
    mean_cross = (sum_cross / width)[:, None]
    back_rows = inv_std * (back_scaled - mean_plain - normed_own * mean_cross)
    input_grad = (chosen_own.astype(jnp.float32) + back_rows).astype(jnp.bfloat16)
    return (block_out, input_grad, grad_in, grad_out, grad_gain, grad_bias)


def solution(mesh):
    placed = (
        P(("rep", "fsdp"), "tp"),
        P(("rep", "fsdp"), "tp"),
        P(("rep", "fsdp")),
        P("tp"),
        P("tp"),
        P("fsdp", "tp"),
        P("tp", "fsdp"),
        P("fsdp", "tp"),
        P("tp", "fsdp"),
    )
    return jax.shard_map(
        partial(on_device, dict(mesh.shape)),
        mesh=mesh,
        in_specs=placed,
        out_specs=(
            P(("rep", "fsdp"), "tp"),
            P(("rep", "fsdp"), "tp"),
            P("fsdp", "tp"),
            P("tp", "fsdp"),
            P("tp"),
            P("tp"),
        ),
        check_vma=False,
    )
```

```python
from functools import partial

import jax
import jax.numpy as jnp
from jax import lax
from jax.sharding import PartitionSpec as P

BLK = 128


def apply_blocks(weight, blocks, kind):
    row_blocks, col_blocks = blocks.shape
    shaped = weight.reshape(row_blocks, BLK, col_blocks, BLK)
    keeper = blocks.astype(kind)[:, None, :, None]
    return (shaped * keeper).reshape(weight.shape)


def contract_rows(left, right):
    return lax.dot_general(
        left, right, (((0,), (0,)), ((), ())), preferred_element_type=jnp.float32
    )


def contract_cols(left, right):
    return lax.dot_general(
        left, right, (((1,), (1,)), ((), ())), preferred_element_type=jnp.float32
    )


def pair_gather(own, axis):
    other = lax.ppermute(own, "fsdp", perm=[(0, 1), (1, 0)])
    first = lax.axis_index("fsdp") == 0
    low = jnp.where(first, own, other)
    high = jnp.where(first, other, own)
    return jnp.concatenate([low, high], axis=axis)


def pair_scatter(term, axis):
    half = term.shape[axis] // 2
    idx = lax.axis_index("fsdp")
    keep = lax.dynamic_slice_in_dim(term, idx * half, half, axis)
    send = lax.dynamic_slice_in_dim(term, (1 - idx) * half, half, axis)
    recv = lax.ppermute(send, "fsdp", perm=[(0, 1), (1, 0)])
    return keep.astype(jnp.float32) + recv.astype(jnp.float32)


def rows_allreduce(term, axis, size):
    rows = term.shape[0] // size
    mine = lax.all_to_all(term.astype(jnp.bfloat16), axis, split_axis=0, concat_axis=0, tiled=True)
    reduced = jnp.sum(mine.reshape(size, rows, -1).astype(jnp.float32), axis=0)
    reduced = reduced.astype(jnp.bfloat16)
    copies = jnp.broadcast_to(reduced[None], (size,) + reduced.shape).reshape(term.shape)
    whole = lax.all_to_all(copies, axis, split_axis=0, concat_axis=0, tiled=True)
    return whole.astype(jnp.float32)


def butterfly_sum(values, axis, size):
    bit = 1
    while bit < size:
        perm = [(i, i ^ bit) for i in range(size)]
        values = values + lax.ppermute(values, axis, perm=perm)
        bit *= 2
    return values


def on_device(
    sizes,
    tokens, cotangent, frame_mask, ln_gain, ln_bias, weight_in, weight_out, blocks_in, blocks_out
):
    frames = tokens.shape[0]
    stacked = jnp.concatenate(
        [tokens, ln_gain[None], ln_bias[None], jnp.zeros((6, tokens.shape[1]), tokens.dtype)]
    )
    gathered = lax.all_to_all(
        jnp.tile(stacked, (1, sizes["tp"])), "tp", split_axis=1, concat_axis=1, tiled=True
    )
    whole_rows = gathered[:frames]
    gain_full, bias_full = gathered[frames], gathered[frames + 1]
    masked_in = apply_blocks(weight_in, blocks_in, jnp.bfloat16)
    masked_out = apply_blocks(weight_out, blocks_out, jnp.bfloat16)
    full_in = pair_gather(masked_in, 0)
    full_out = pair_gather(masked_out, 1)
    width = whole_rows.shape[1]
    own_width = tokens.shape[1]
    col_start = lax.axis_index("tp") * own_width
    gelu_exact = partial(jax.nn.gelu, approximate=False)
    values = whole_rows.astype(jnp.float32)
    centre = jnp.mean(values, axis=1, keepdims=True)
    centred = values - centre
    inv_std = lax.rsqrt(jnp.mean(centred * centred, axis=1, keepdims=True) + 1e-05)
    normed = centred * inv_std
    gain_f = gain_full.astype(jnp.float32)
    scaled = (normed * gain_f + bias_full.astype(jnp.float32)).astype(jnp.bfloat16)
    hidden = jnp.dot(scaled, full_in, preferred_element_type=jnp.float32)
    active = gelu_exact(hidden).astype(jnp.bfloat16)
    partial_out = lax.dot_general(
        full_out, active, (((0,), (1,)), ((), ())), preferred_element_type=jnp.float32
    ).astype(jnp.bfloat16)
    whole_grad = lax.all_gather(cotangent, "tp", axis=1, tiled=True)
    unused, whole_grad = lax.optimization_barrier((partial_out, whole_grad))
    branch = lax.psum_scatter(
        partial_out, "tp", scatter_dimension=0, tiled=True
    ).astype(jnp.float32).T
    flags = frame_mask[:, None].astype(jnp.bfloat16)
    chosen = whole_grad * flags
    chosen_own = cotangent * flags
    back_active = contract_cols(chosen, full_out)
    unused, gelu_back = jax.vjp(gelu_exact, hidden)
    back_hidden = gelu_back(back_active)[0].astype(jnp.bfloat16)
    partial_normed = contract_cols(back_hidden, full_in).astype(jnp.bfloat16)
    back_normed = lax.psum_scatter(
        partial_normed, "tp", scatter_dimension=1, tiled=True
    ).astype(jnp.float32)
    piece = partial_normed.astype(jnp.float32)
    piece_scaled = piece * gain_f
    row_sums = jnp.stack([jnp.sum(piece_scaled, axis=1), jnp.sum(piece_scaled * normed, axis=1)])
    col_sums = jnp.stack([jnp.sum(piece * normed, axis=0), jnp.sum(piece, axis=0)])
    both_sums = butterfly_sum(jnp.concatenate([row_sums, col_sums], axis=1), "tp", sizes["tp"])
    row_sums, col_sums = both_sums[:, :frames], both_sums[:, frames:]
    sum_plain, sum_cross = row_sums[0], row_sums[1]
    for name in ("fsdp", "rep"):
        col_sums = butterfly_sum(col_sums, name, sizes[name])
    whole_gain, whole_bias = col_sums[0], col_sums[1]
    grad_gain = lax.dynamic_slice_in_dim(whole_gain, col_start, own_width, 0)
    grad_bias = lax.dynamic_slice_in_dim(whole_bias, col_start, own_width, 0)
    term_in = contract_rows(scaled, back_hidden).astype(jnp.bfloat16)
    term_out = contract_rows(active, chosen).astype(jnp.bfloat16)
    shard_in = pair_scatter(term_in, 0)
    shard_out = pair_scatter(term_out, 1)
    shard_in, shard_out, branch = lax.optimization_barrier((shard_in, shard_out, branch))
    block_out = (tokens.astype(jnp.float32) + branch).astype(jnp.bfloat16)
    rows_in = shard_in.shape[0]
    paired = jnp.concatenate([shard_in, shard_out.reshape(rows_in, -1)], axis=1)
    paired = rows_allreduce(paired, "rep", sizes["rep"])
    shard_out = paired[:, shard_in.shape[1]:].reshape(shard_out.shape)
    shard_in = paired[:, : shard_in.shape[1]]
    grad_in = apply_blocks(shard_in, blocks_in, jnp.float32)
    grad_out = apply_blocks(shard_out, blocks_out, jnp.float32)
    grad_in, grad_out, back_normed = lax.optimization_barrier((grad_in, grad_out, back_normed))
    normed_own = lax.dynamic_slice_in_dim(normed, col_start, own_width, 1)
    gain_own = ln_gain.astype(jnp.float32)
    back_scaled = back_normed * gain_own
    mean_plain = (sum_plain / width)[:, None]
    mean_cross = (sum_cross / width)[:, None]
    back_rows = inv_std * (back_scaled - mean_plain - normed_own * mean_cross)
    input_grad = (chosen_own.astype(jnp.float32) + back_rows).astype(jnp.bfloat16)
    return (block_out, input_grad, grad_in, grad_out, grad_gain, grad_bias)


def solution(mesh):
    placed = (
        P(("rep", "fsdp"), "tp"),
        P(("rep", "fsdp"), "tp"),
        P(("rep", "fsdp")),
        P("tp"),
        P("tp"),
        P("fsdp", "tp"),
        P("tp", "fsdp"),
        P("fsdp", "tp"),
        P("tp", "fsdp"),
    )
    return jax.shard_map(
        partial(on_device, dict(mesh.shape)),
        mesh=mesh,
        in_specs=placed,
        out_specs=(
            P(("rep", "fsdp"), "tp"),
            P(("rep", "fsdp"), "tp"),
            P("fsdp", "tp"),
            P("tp", "fsdp"),
            P("tp"),
            P("tp"),
        ),
        check_vma=False,
    )
```
